256 devices in a mesh: rows: 32 (over y, x, core), cols: 8 (over z).
Axes of the slice: x: 4, y: 4, z: 8, core: 2. Of those that a mesh axis runs over, the one named last changes fastest.
Arguments:
- sheet: bfloat16 [16, 4096, 1024], P('cols', 'rows'), may hold values from -600 to 600
- w_in: bfloat16 [1024, 16, 384], P(None, 'cols'), may hold values from -0.1875 to 0.1875
- w_out: bfloat16 [16, 128, 1024], P('cols'), may hold values from -0.125 to 0.125
Outputs:
- mixed: bfloat16 [16, 4096, 1024], P('cols', 'rows')
The draws below stay inside these ranges and needn't reach their ends.
All inputs are finite; a program needn't handle non-finite values.
Results may differ from the reference program's by a relative error of at most 0.0067.
Values may be sent and summed in bfloat16 or wider, within the bound.
No kernel may reach another device: no remote copies, remote signals or barrier semaphores. Data moves between devices by JAX's collectives and lax.ppermute only.
A program may use at most 128 MiB of HBM per device.

```python
import math
import jax
import jax.numpy as jnp
from jax import lax

D = 1024
HEADS = 16
HDIM = 64
ROW_DEV = 128
ROWS = 4096
COLS = 16


def draw_sheet(key, part):
    key_base, key_cell, key_feat = jax.random.split(jax.random.fold_in(key, 11), 3)
    base = jnp.clip(jax.random.normal(key_base, (COLS, ROWS, D), jnp.float32), -6.0, 6.0)
    cell_scale = jnp.exp(jax.random.uniform(key_cell, (COLS, ROWS, 1), jnp.float32, 0.0, math.log(10.0)))
    feat_scale = jnp.exp(jax.random.uniform(key_feat, (1, 1, D), jnp.float32, 0.0, math.log(10.0)))
    return (base * cell_scale * feat_scale).astype(jnp.bfloat16)


def level_of(stream_key, dims, cuts, smallest, largest):
    gain, own = 1.0, jax.random.fold_in(stream_key, 6)
    for axis_at, shards_of in cuts:
        steps = jnp.exp(jax.random.uniform(jax.random.fold_in(own, axis_at), (shards_of,), jnp.float32, smallest / len(cuts), largest / len(cuts)))
        gain = gain * jnp.repeat(steps, dims[axis_at] // shards_of).reshape([-1 if axis == axis_at else 1 for axis in range(len(dims))])
    return gain


def gaussian(stream_key, extent, deviation, bound, cuts=(), dtype=jnp.bfloat16):
    level = level_of(stream_key, extent, cuts, -0.22, 0.18) if cuts else 1.0
    entries = jax.random.normal(stream_key, extent, jnp.float32) * deviation * level
    return jnp.minimum(jnp.maximum(entries, -bound), bound).astype(dtype)


def setup_inputs(seed: int = 0) -> dict:
    seeds = jax.random.split(jax.random.key(seed), 4)
    return {
        "sheet": draw_sheet(jax.random.fold_in(seeds[3], 71), 0),
        "w_in": gaussian(seeds[1], (D, HEADS, 6 * HDIM), D ** -0.5, 0.1875, ((1, 8),)),
        "w_out": gaussian(seeds[2], (HEADS, 2 * HDIM, D), (2 * D) ** -0.5, 0.125, ((0, 8),)),
    }


def head_norm(values):
    return values * lax.rsqrt(lax.optimization_barrier(jnp.mean(values * values, axis=-1, keepdims=True)) + 1e-06)

def feature_map(values):
    return jax.nn.elu(values) + 1.0

def finish_proj(proj):
    parts = [head_norm(proj[..., 0, :]), head_norm(proj[..., 1, :]), proj[..., 2, :], feature_map(proj[..., 3, :]), feature_map(proj[..., 4, :]), proj[..., 5, :]]
    return jnp.stack(parts, axis=-2).astype(jnp.bfloat16)

def reference(sheet, w_in, w_out):
    high = lax.Precision.HIGHEST
    xfull = sheet.astype(jnp.float32)
    normed = (xfull * lax.rsqrt(lax.optimization_barrier(jnp.mean(xfull * xfull, axis=-1, keepdims=True)) + 1e-06)).astype(jnp.bfloat16)
    flat = normed.reshape(COLS * ROWS, D)
    scale = HDIM ** (-0.5)
    blocks = ROWS // ROW_DEV
    causal = (jnp.arange(ROW_DEV)[:, None] >= jnp.arange(ROW_DEV)[None, :]).astype(jnp.float32)

    def one_head(total, inputs):
        w_head, w_back = inputs
        proj = jnp.dot(flat, w_head, preferred_element_type=jnp.float32).reshape(COLS, ROWS, 6, HDIM)
        parts = finish_proj(proj).astype(jnp.float32)
        qrow, krow, vrow = (parts[:, :, 0], parts[:, :, 1], parts[:, :, 2])
        fq, fk, vcol = (parts[:, :, 3], parts[:, :, 4], parts[:, :, 5])
        score = jnp.einsum('crd,erd->rce', qrow, krow) * scale
        expo = jnp.exp(score)
        weights = (expo / lax.optimization_barrier(jnp.sum(expo, axis=-1, keepdims=True))).astype(jnp.bfloat16)
        orow = jnp.einsum('rce,erd->crd', weights.astype(jnp.float32), vrow).astype(jnp.bfloat16)
        fqb = fq.reshape(COLS, blocks, ROW_DEV, HDIM)
        fkb = fk.reshape(COLS, blocks, ROW_DEV, HDIM)
        vcb = vcol.reshape(COLS, blocks, ROW_DEV, HDIM)
        states = jnp.einsum('cbsk,cbsv->cbkv', fkb, vcb, precision=high)
        running = jnp.cumsum(states, axis=1)
        prior = jnp.concatenate([jnp.zeros_like(running[:, :1]), running[:, :-1]], axis=1)
        carried = jnp.einsum('cbtk,cbkv->cbtv', fqb, prior, precision=high)
        inner = jnp.einsum('cbtd,cbsd->cbts', fqb, fkb, precision=high) * causal
        local = jnp.einsum('cbts,cbsv->cbtv', inner, vcb, precision=high)
        pre = (carried + local).reshape(COLS, ROWS, HDIM)
        ocol = head_norm(pre).astype(jnp.bfloat16)
        both = jnp.concatenate([orow, ocol], axis=-1).reshape(COLS * ROWS, 2 * HDIM)
        return (total + jnp.dot(both, w_back, preferred_element_type=jnp.float32), None)
    start = jnp.zeros((COLS * ROWS, D), jnp.float32)
    total, unused = lax.scan(one_head, start, (jnp.moveaxis(w_in, 1, 0), w_out))
    return total.reshape(COLS, ROWS, D).astype(jnp.bfloat16)
```

```python
import jax
import jax.numpy as jnp
import numpy as np
from jax import lax
from jax.sharding import Mesh, PartitionSpec as P

ROWS_AXES = ("y", "x", "core")


def head_norm(values):
    return values * lax.rsqrt(jnp.mean(values * values, axis=-1, keepdims=True) + 1e-06)


def feature_map(values):
    return jax.nn.elu(values) + 1.0


def finish_proj(proj):
    parts = [
        head_norm(proj[..., 0, :]),
        head_norm(proj[..., 1, :]),
        proj[..., 2, :],
        feature_map(proj[..., 3, :]),
        feature_map(proj[..., 4, :]),
        proj[..., 5, :],
    ]
    return jnp.stack(parts, axis=-2).astype(jnp.bfloat16)


def masked_prefix(gathered, mine):
    idx = lax.broadcasted_iota(jnp.int32, gathered.shape, 0)
    before = jnp.sum(jnp.where(idx < mine, gathered, 0.0), axis=0)
    return before, jnp.sum(gathered, axis=0)


def exclusive_rows_scan(states):
    core = lax.axis_index("core")
    pair = lax.all_gather(states, "core")
    total = pair[0] + pair[1]
    own = jnp.where(core == 1, pair[0], jnp.zeros_like(pair[0]))
    half = total.shape[0] // 2
    mine = lax.dynamic_slice_in_dim(total, core * half, half, axis=0)
    gx = lax.all_gather(mine, "x")
    xpre, xsum = masked_prefix(gx, lax.axis_index("x"))
    gy = lax.all_gather(xsum, "y")
    ypre, _ = masked_prefix(gy, lax.axis_index("y"))
    chip_prefix = lax.all_gather(ypre + xpre, "core", axis=0, tiled=True)
    return chip_prefix + own


def body(sheet, w_in, w_out):
    high = lax.Precision.HIGHEST
    width = sheet.shape[2]
    heads_here = w_in.shape[1]
    hdim = w_out.shape[1] // 2
    ncols = lax.axis_size("cols")
    core = lax.axis_index("core")

    wh = width // 2
    w_part = lax.dynamic_slice_in_dim(w_out, core * wh, wh, axis=2)
    w_part = lax.all_gather(w_part, "cols", axis=0, tiled=True)
    w_full = lax.all_gather(w_part, "core", axis=2, tiled=True)

    xloc = sheet.astype(jnp.float32)
    normed = (xloc * lax.rsqrt(jnp.mean(xloc * xloc, axis=-1, keepdims=True) + 1e-06)).astype(jnp.bfloat16)
    piece = lax.all_gather(normed, "cols", axis=0, tiled=True)

    w_flat = w_in.reshape(width, heads_here * 6 * hdim)
    proj = jnp.dot(piece.reshape(-1, width), w_flat, preferred_element_type=jnp.float32)
    all_cols, row_count = piece.shape[0], piece.shape[1]
    parts = finish_proj(proj.reshape(all_cols, row_count, heads_here, 6, hdim))
    qrow, krow, vrow = (parts[:, :, :, 0], parts[:, :, :, 1], parts[:, :, :, 2])
    fq, fk, vcol = (parts[:, :, :, 3], parts[:, :, :, 4], parts[:, :, :, 5])

    states = jnp.einsum("crhk,crhv->chkv", fk, vcol, preferred_element_type=jnp.float32)
    prior = exclusive_rows_scan(states)

    scale = hdim ** (-0.5)
    score = jnp.einsum("crhd,erhd->rhce", qrow, krow, preferred_element_type=jnp.float32) * scale
    expo = jnp.exp(score)
    weights = (expo / jnp.sum(expo, axis=-1, keepdims=True)).astype(jnp.bfloat16)
    orow = jnp.einsum("rhce,erhd->crhd", weights, vrow, preferred_element_type=jnp.float32).astype(jnp.bfloat16)

    causal = (jnp.arange(row_count)[:, None] >= jnp.arange(row_count)[None, :]).astype(jnp.float32)
    inner = jnp.einsum("cthd,cshd->chts", fq, fk, preferred_element_type=jnp.float32) * causal
    local = jnp.einsum("chts,cshv->cthv", inner, vcol.astype(jnp.float32), precision=high)
    carried = jnp.einsum("cthk,chkv->cthv", fq.astype(jnp.float32), prior, precision=high)
    ocol = head_norm(carried + local).astype(jnp.bfloat16)

    results = jnp.concatenate([orow, ocol], axis=3)
    mine = lax.all_to_all(results, "cols", 0, 2, tiled=True)
    own_cols = mine.shape[0]
    mixed = jnp.dot(
        mine.reshape(own_cols * row_count, -1),
        w_full.reshape(-1, width),
        preferred_element_type=jnp.float32,
    )
    return mixed.reshape(own_cols, row_count, width).astype(jnp.bfloat16)


def split_mesh(mesh):
    devs = mesh.devices
    n_rows, n_cols = devs.shape
    try:
        nx = len({d.coords[0] for d in devs.flat})
    except Exception:
        nx = 4
    ny = n_rows // (nx * 2)
    return Mesh(devs.reshape(ny, nx, 2, n_cols), ROWS_AXES + ("cols",))


def solution(mesh):
    m4 = split_mesh(mesh)
    spec = P("cols", ROWS_AXES, None)
    return jax.shard_map(
        body,
        mesh=m4,
        in_specs=(spec, P(None, "cols", None), P("cols", None, None)),
        out_specs=spec,
        check_vma=False,
    )
```

```python
import jax
import jax.numpy as jnp
import numpy as np
from jax import lax
from jax.sharding import Mesh, PartitionSpec as P

ROWS_AXES = ("y", "x", "core")


def head_norm(values):
    return values * lax.rsqrt(jnp.mean(values * values, axis=-1, keepdims=True) + 1e-06)


def feature_map(values):
    return jax.nn.elu(values) + 1.0


def finish_proj(proj):
    parts = [
        head_norm(proj[..., 0, :]),
        head_norm(proj[..., 1, :]),
        proj[..., 2, :],
        feature_map(proj[..., 3, :]),
        feature_map(proj[..., 4, :]),
        proj[..., 5, :],
    ]
    return jnp.stack(parts, axis=-2).astype(jnp.bfloat16)


def recv_from(v, axis, k):
    n = lax.axis_size(axis)
    return lax.ppermute(v, axis, [(i, (i + k) % n) for i in range(n)])


def line_prefix(v, axis):
    n = lax.axis_size(axis)
    me = lax.axis_index(axis)
    before = jnp.zeros_like(v)
    total = v
    for k in range(1, n):
        got = recv_from(v, axis, k)
        before = before + jnp.where(k <= me, got, jnp.zeros_like(got))
        total = total + got
    return before, total


def exclusive_rows_scan(states):
    core = lax.axis_index("core")
    other = recv_from(states, "core", 1)
    total = states + other
    own = jnp.where(core == 1, other, jnp.zeros_like(other))
    half = total.shape[0] // 2
    mine = lax.dynamic_slice_in_dim(total, core * half, half, axis=0)
    xpre, xsum = line_prefix(mine, "x")
    ypre, _ = line_prefix(xsum, "y")
    part = ypre + xpre
    part_other = recv_from(part, "core", 1)
    lo = jnp.where(core == 0, part, part_other)
    hi = jnp.where(core == 0, part_other, part)
    return jnp.concatenate([lo, hi], axis=0) + own


def to_owners(res):
    n = lax.axis_size("cols")
    g = lax.axis_index("cols")
    blocks = res.reshape(n, res.shape[0] // n, *res.shape[1:])
    got = [blocks[g]]
    for k in range(1, n):
        send = lax.dynamic_index_in_dim(blocks, (g + k) % n, axis=0, keepdims=False)
        got.append(recv_from(send, "cols", k))
    stacked = jnp.stack(got)
    order = (g - jnp.arange(n)) % n
    return jnp.take(stacked, order, axis=0)


def body(sheet, w_in, w_out):
    high = lax.Precision.HIGHEST
    width = sheet.shape[2]
    heads_here = w_in.shape[1]
    hdim = w_out.shape[1] // 2
    core = lax.axis_index("core")

    w_mine = lax.all_gather(lax.dynamic_index_in_dim(w_out, core, axis=0, keepdims=False), "cols")
    w_other = recv_from(w_mine, "core", 1)

    xloc = sheet.astype(jnp.float32)
    normed = (xloc * lax.rsqrt(jnp.mean(xloc * xloc, axis=-1, keepdims=True) + 1e-06)).astype(jnp.bfloat16)
    piece = lax.all_gather(normed, "cols", axis=0, tiled=True)

    w_flat = w_in.reshape(width, heads_here * 6 * hdim)
    proj = jnp.dot(piece.reshape(-1, width), w_flat, preferred_element_type=jnp.float32)
    all_cols, row_count = piece.shape[0], piece.shape[1]
    parts = finish_proj(proj.reshape(all_cols, row_count, heads_here, 6, hdim))
    qrow, krow, vrow = (parts[:, :, :, 0], parts[:, :, :, 1], parts[:, :, :, 2])
    fq, fk, vcol = (parts[:, :, :, 3], parts[:, :, :, 4], parts[:, :, :, 5])

    states = jnp.einsum("crhk,crhv->chkv", fk, vcol, preferred_element_type=jnp.float32)
    prior = exclusive_rows_scan(states)

    scale = hdim ** (-0.5)
    score = jnp.einsum("crhd,erhd->rhce", qrow, krow, preferred_element_type=jnp.float32) * scale
    expo = jnp.exp(score)
    weights = (expo / jnp.sum(expo, axis=-1, keepdims=True)).astype(jnp.bfloat16)
    orow = jnp.einsum("rhce,erhd->crhd", weights, vrow, preferred_element_type=jnp.float32).astype(jnp.bfloat16)
    orow_all = to_owners(orow)

    causal = (jnp.arange(row_count)[:, None] >= jnp.arange(row_count)[None, :]).astype(jnp.float32)
    inner = jnp.einsum("cthd,cshd->chts", fq, fk, preferred_element_type=jnp.float32) * causal
    local = jnp.einsum("chts,cshv->cthv", inner, vcol.astype(jnp.float32), precision=high)
    carried = jnp.einsum("cthk,chkv->cthv", fq.astype(jnp.float32), prior, precision=high)
    ocol = head_norm(carried + local).astype(jnp.bfloat16)
    ocol_all = to_owners(ocol)

    other_head = 1 - core

    def project(vals, w, head):
        v = lax.dynamic_index_in_dim(vals, head, axis=3, keepdims=False)
        return jnp.einsum("scrf,sfn->crn", v, w, preferred_element_type=jnp.float32)

    mixed = (
        project(orow_all, w_mine[:, :hdim], core)
        + project(ocol_all, w_mine[:, hdim:], core)
    ) + (
        project(orow_all, w_other[:, :hdim], other_head)
        + project(ocol_all, w_other[:, hdim:], other_head)
    )
    return mixed.astype(jnp.bfloat16)


def split_mesh(mesh):
    devs = mesh.devices
    n_rows, n_cols = devs.shape
    try:
        nx = len({d.coords[0] for d in devs.flat})
    except Exception:
        nx = 4
    ny = n_rows // (nx * 2)
    return Mesh(devs.reshape(ny, nx, 2, n_cols), ROWS_AXES + ("cols",))


def solution(mesh):
    m4 = split_mesh(mesh)
    spec = P("cols", ROWS_AXES, None)
    return jax.shard_map(
        body,
        mesh=m4,
        in_specs=(spec, P(None, "cols", None), P("cols", None, None)),
        out_specs=spec,
        check_vma=False,
    )
```

```python
import jax
import jax.numpy as jnp
import numpy as np
from jax import lax
from jax.sharding import Mesh, PartitionSpec as P

ROWS_AXES = ("y", "x", "core")


def head_norm(values):
    return values * lax.rsqrt(jnp.mean(values * values, axis=-1, keepdims=True) + 1e-06)


def feature_map(values):
    return jax.nn.elu(values) + 1.0


def finish_proj(proj):
    parts = [
        head_norm(proj[..., 0, :]),
        head_norm(proj[..., 1, :]),
        proj[..., 2, :],
        feature_map(proj[..., 3, :]),
        feature_map(proj[..., 4, :]),
        proj[..., 5, :],
    ]
    return jnp.stack(parts, axis=-2).astype(jnp.bfloat16)


def recv_from(v, axis, k):
    n = lax.axis_size(axis)
    return lax.ppermute(v, axis, [(i, (i + k) % n) for i in range(n)])


def line_prefix(v, axis):
    n = lax.axis_size(axis)
    me = lax.axis_index(axis)
    before = jnp.zeros_like(v)
    total = v
    for k in range(1, n):
        got = recv_from(v, axis, k)
        before = before + jnp.where(k <= me, got, jnp.zeros_like(got))
        total = total + got
    return before, total


def exclusive_rows_scan(states, held):
    core = lax.axis_index("core")
    other = recv_from(states, "core", 1)
    other, held = lax.optimization_barrier((other, held))
    total = states + other
    own = jnp.where(core == 1, other, jnp.zeros_like(other))
    half = total.shape[0] // 2
    mine = lax.dynamic_slice_in_dim(total, core * half, half, axis=0)
    xpre, xsum = line_prefix(mine, "x")
    ypre, _ = line_prefix(xsum, "y")
    part = ypre + xpre
    part_other = recv_from(part, "core", 1)
    lo = jnp.where(core == 0, part, part_other)
    hi = jnp.where(core == 0, part_other, part)
    return (jnp.concatenate([lo, hi], axis=0) + own, *held)


def to_owners(res):
    n = lax.axis_size("cols")
    g = lax.axis_index("cols")
    blocks = res.reshape(n, res.shape[0] // n, *res.shape[1:])
    got = [blocks[g]]
    for k in range(1, n):
        send = lax.dynamic_index_in_dim(blocks, (g + k) % n, axis=0, keepdims=False)
        got.append(recv_from(send, "cols", k))
    stacked = jnp.stack(got)
    order = (g - jnp.arange(n)) % n
    return jnp.take(stacked, order, axis=0)


def body(sheet, w_in, w_out):
    high = lax.Precision.HIGHEST
    width = sheet.shape[2]
    heads_here = w_in.shape[1]
    hdim = w_out.shape[1] // 2
    core = lax.axis_index("core")

    xloc = sheet.astype(jnp.float32)
    normed = (xloc * lax.rsqrt(jnp.mean(xloc * xloc, axis=-1, keepdims=True) + 1e-06)).astype(jnp.bfloat16)
    piece = lax.all_gather(normed, "cols", axis=0, tiled=True)

    w_head = lax.dynamic_index_in_dim(w_out, core, axis=0, keepdims=False)
    piece, w_head = lax.optimization_barrier((piece, w_head))
    w_mine = lax.all_gather(w_head, "cols")
    w_other = recv_from(w_mine, "core", 1)

    w_flat = w_in.reshape(width, heads_here * 6 * hdim)
    proj = jnp.dot(piece.reshape(-1, width), w_flat, preferred_element_type=jnp.float32)
    all_cols, row_count = piece.shape[0], piece.shape[1]
    parts = finish_proj(proj.reshape(all_cols, row_count, heads_here, 6, hdim))
    qrow, krow, vrow = (parts[:, :, :, 0], parts[:, :, :, 1], parts[:, :, :, 2])
    fq, fk, vcol = (parts[:, :, :, 3], parts[:, :, :, 4], parts[:, :, :, 5])

    states = jnp.einsum("crhk,crhv->chkv", fk, vcol, preferred_element_type=jnp.float32)
    prior, qrow, krow, vrow = exclusive_rows_scan(states, (qrow, krow, vrow))

    scale = hdim ** (-0.5)
    score = jnp.einsum("crhd,erhd->rhce", qrow, krow, preferred_element_type=jnp.float32) * scale
    expo = jnp.exp(score)
    weights = (expo / jnp.sum(expo, axis=-1, keepdims=True)).astype(jnp.bfloat16)
    orow = jnp.einsum("rhce,erhd->crhd", weights, vrow, preferred_element_type=jnp.float32).astype(jnp.bfloat16)
    orow_all = to_owners(orow)

    causal = (jnp.arange(row_count)[:, None] >= jnp.arange(row_count)[None, :]).astype(jnp.float32)
    inner = jnp.einsum("cthd,cshd->chts", fq, fk, preferred_element_type=jnp.float32) * causal
    local = jnp.einsum("chts,cshv->cthv", inner, vcol.astype(jnp.float32), precision=high)
    carried = jnp.einsum("cthk,chkv->cthv", fq.astype(jnp.float32), prior, precision=high)
    ocol = head_norm(carried + local).astype(jnp.bfloat16)
    ocol_all = to_owners(ocol)

    other_head = 1 - core

    def project(vals, w, head):
        v = lax.dynamic_index_in_dim(vals, head, axis=3, keepdims=False)
        return jnp.einsum("scrf,sfn->crn", v, w, preferred_element_type=jnp.float32)

    mixed = (
        project(orow_all, w_mine[:, :hdim], core)
        + project(ocol_all, w_mine[:, hdim:], core)
    ) + (
        project(orow_all, w_other[:, :hdim], other_head)
        + project(ocol_all, w_other[:, hdim:], other_head)
    )
    return mixed.astype(jnp.bfloat16)


def split_mesh(mesh):
    devs = mesh.devices
    n_rows, n_cols = devs.shape
    try:
        nx = len({d.coords[0] for d in devs.flat})
    except Exception:
        nx = 4
    ny = n_rows // (nx * 2)
    return Mesh(devs.reshape(ny, nx, 2, n_cols), ROWS_AXES + ("cols",))


def solution(mesh):
    m4 = split_mesh(mesh)
    spec = P("cols", ROWS_AXES, None)
    return jax.shard_map(
        body,
        mesh=m4,
        in_specs=(spec, P(None, "cols", None), P("cols", None, None)),
        out_specs=spec,
        check_vma=False,
    )
```

```python
import jax
import jax.numpy as jnp
import numpy as np
from jax import lax
from jax.sharding import Mesh, PartitionSpec as P

ROWS_AXES = ("y", "x", "core")


def head_norm(values):
    return values * lax.rsqrt(jnp.mean(values * values, axis=-1, keepdims=True) + 1e-06)


def feature_map(values):
    return jax.nn.elu(values) + 1.0


def finish_proj(proj):
    parts = [
        head_norm(proj[..., 0, :]),
        head_norm(proj[..., 1, :]),
        proj[..., 2, :],
        feature_map(proj[..., 3, :]),
        feature_map(proj[..., 4, :]),
        proj[..., 5, :],
    ]
    return jnp.stack(parts, axis=-2).astype(jnp.bfloat16)


def recv_from(v, axis, k):
    n = lax.axis_size(axis)
    return lax.ppermute(v, axis, [(i, (i + k) % n) for i in range(n)])


def line_prefix(v, axis, held=None):
    n = lax.axis_size(axis)
    me = lax.axis_index(axis)
    sent = v.astype(jnp.bfloat16)
    got = [recv_from(sent, axis, k) for k in range(1, n)]
    got, held = lax.optimization_barrier((got, held))
    before = jnp.zeros_like(v)
    total = v
    for k, g in enumerate(got, start=1):
        g = g.astype(v.dtype)
        before = before + jnp.where(k <= me, g, jnp.zeros_like(g))
        total = total + g
    return before, total, held


def exclusive_rows_scan(states, inputs, work):
    core = lax.axis_index("core")
    other = recv_from(states, "core", 1)
    other, inputs = lax.optimization_barrier((other, inputs))
    done = work(*inputs)
    total = states + other
    own = jnp.where(core == 1, other, jnp.zeros_like(other))
    half = total.shape[0] // 2
    mine = lax.dynamic_slice_in_dim(total, core * half, half, axis=0)
    xpre, xsum, done = line_prefix(mine, "x", done)
    ypre, _, _ = line_prefix(xsum, "y")
    part = ypre + xpre
    part_other = recv_from(part, "core", 1)
    lo = jnp.where(core == 0, part, part_other)
    hi = jnp.where(core == 0, part_other, part)
    return jnp.concatenate([lo, hi], axis=0) + own, done


def to_owners(res):
    n = lax.axis_size("cols")
    g = lax.axis_index("cols")
    blocks = res.reshape(n, res.shape[0] // n, *res.shape[1:])
    got = [blocks[g]]
    for k in range(1, n):
        send = lax.dynamic_index_in_dim(blocks, (g + k) % n, axis=0, keepdims=False)
        got.append(recv_from(send, "cols", k))
    stacked = jnp.stack(got)
    order = (g - jnp.arange(n)) % n
    return jnp.take(stacked, order, axis=0)


def body(sheet, w_in, w_out):
    high = lax.Precision.HIGHEST
    width = sheet.shape[2]
    heads_here = w_in.shape[1]
    hdim = w_out.shape[1] // 2
    core = lax.axis_index("core")

    xloc = sheet.astype(jnp.float32)
    normed = (xloc * lax.rsqrt(jnp.mean(xloc * xloc, axis=-1, keepdims=True) + 1e-06)).astype(jnp.bfloat16)
    piece = lax.all_gather(normed, "cols", axis=0, tiled=True)

    w_head = lax.dynamic_index_in_dim(w_out, core, axis=0, keepdims=False)
    piece, w_head = lax.optimization_barrier((piece, w_head))
    w_mine = lax.all_gather(w_head, "cols")
    w_other = recv_from(w_mine, "core", 1)

    w_flat = w_in.reshape(width, heads_here * 6 * hdim)
    proj = jnp.dot(piece.reshape(-1, width), w_flat, preferred_element_type=jnp.float32)
    all_cols, row_count = piece.shape[0], piece.shape[1]
    parts = finish_proj(proj.reshape(all_cols, row_count, heads_here, 6, hdim))
    qrow, krow, vrow = (parts[:, :, :, 0], parts[:, :, :, 1], parts[:, :, :, 2])
    fq, fk, vcol = (parts[:, :, :, 3], parts[:, :, :, 4], parts[:, :, :, 5])

    states = jnp.einsum("crhk,crhv->chkv", fk, vcol, preferred_element_type=jnp.float32)
    scale = hdim ** (-0.5)

    def row_attention(qrow, krow, vrow):
        score = jnp.einsum("crhd,erhd->rhce", qrow, krow, preferred_element_type=jnp.float32) * scale
        expo = jnp.exp(score)
        weights = (expo / jnp.sum(expo, axis=-1, keepdims=True)).astype(jnp.bfloat16)
        return jnp.einsum("rhce,erhd->crhd", weights, vrow, preferred_element_type=jnp.float32).astype(
            jnp.bfloat16
        )

    prior, orow = exclusive_rows_scan(states, (qrow, krow, vrow), row_attention)
    orow_all = to_owners(orow)

    causal = (jnp.arange(row_count)[:, None] >= jnp.arange(row_count)[None, :]).astype(jnp.float32)
    inner = jnp.einsum("cthd,cshd->chts", fq, fk, preferred_element_type=jnp.float32) * causal
    local = jnp.einsum("chts,cshv->cthv", inner, vcol.astype(jnp.float32), precision=high)
    carried = jnp.einsum("cthk,chkv->cthv", fq.astype(jnp.float32), prior, precision=high)
    ocol = head_norm(carried + local).astype(jnp.bfloat16)
    ocol_all = to_owners(ocol)

    other_head = 1 - core

    def project(vals, w, head):
        v = lax.dynamic_index_in_dim(vals, head, axis=3, keepdims=False)
        return jnp.einsum("scrf,sfn->crn", v, w, preferred_element_type=jnp.float32)

    mixed = (
        project(orow_all, w_mine[:, :hdim], core)
        + project(ocol_all, w_mine[:, hdim:], core)
    ) + (
        project(orow_all, w_other[:, :hdim], other_head)
        + project(ocol_all, w_other[:, hdim:], other_head)
    )
    return mixed.astype(jnp.bfloat16)


def split_mesh(mesh):
    devs = mesh.devices
    n_rows, n_cols = devs.shape
    try:
        nx = len({d.coords[0] for d in devs.flat})
    except Exception:
        nx = 4
    ny = n_rows // (nx * 2)
    return Mesh(devs.reshape(ny, nx, 2, n_cols), ROWS_AXES + ("cols",))


def solution(mesh):
    m4 = split_mesh(mesh)
    spec = P("cols", ROWS_AXES, None)
    return jax.shard_map(
        body,
        mesh=m4,
        in_specs=(spec, P(None, "cols", None), P("cols", None, None)),
        out_specs=spec,
        check_vma=False,
    )
```

```python
import jax
import jax.numpy as jnp
import numpy as np
from jax import lax
from jax.sharding import Mesh, PartitionSpec as P

ROWS_AXES = ("y", "x", "core")


def head_norm(values):
    return values * lax.rsqrt(jnp.mean(values * values, axis=-1, keepdims=True) + 1e-06)


def feature_map(values):
    return jax.nn.elu(values) + 1.0


def recv_from(v, axis, k):
    n = lax.axis_size(axis)
    return lax.ppermute(v, axis, [(i, (i + k) % n) for i in range(n)])


def line_prefix(v, axis, held=None):
    n = lax.axis_size(axis)
    me = lax.axis_index(axis)
    sent = v.astype(jnp.bfloat16)
    got = [recv_from(sent, axis, k) for k in range(1, n)]
    got, held = lax.optimization_barrier((got, held))
    before = jnp.zeros_like(v)
    total = v
    for k, g in enumerate(got, start=1):
        g = g.astype(v.dtype)
        before = before + jnp.where(k <= me, g, jnp.zeros_like(g))
        total = total + g
    return before, total, held


def exclusive_rows_scan(states, inputs, x_work, y_work):
    core = lax.axis_index("core")
    other = recv_from(states, "core", 1)
    other, inputs = lax.optimization_barrier((other, inputs))
    xdone = x_work(*inputs)
    total = states + other
    own = jnp.where(core == 1, other, jnp.zeros_like(other))
    half = total.shape[0] // 2
    mine = lax.dynamic_slice_in_dim(total, core * half, half, axis=0)
    xpre, xsum, xdone = line_prefix(mine, "x", xdone)
    ydone = y_work(*xdone)
    ypre, _, ydone = line_prefix(xsum, "y", ydone)
    part = ypre + xpre
    part_other = recv_from(part, "core", 1)
    lo = jnp.where(core == 0, part, part_other)
    hi = jnp.where(core == 0, part_other, part)
    return jnp.concatenate([lo, hi], axis=0) + own, ydone


def to_owners(res):
    n = lax.axis_size("cols")
    g = lax.axis_index("cols")
    blocks = res.reshape(n, res.shape[0] // n, *res.shape[1:])
    got = [blocks[g]]
    for k in range(1, n):
        send = lax.dynamic_index_in_dim(blocks, (g + k) % n, axis=0, keepdims=False)
        got.append(recv_from(send, "cols", k))
    stacked = jnp.stack(got)
    order = (g - jnp.arange(n)) % n
    return jnp.take(stacked, order, axis=0)


def body(sheet, w_in, w_out):
    high = lax.Precision.HIGHEST
    width = sheet.shape[2]
    heads_here = w_in.shape[1]
    hdim = w_out.shape[1] // 2
    core = lax.axis_index("core")

    xloc = sheet.astype(jnp.float32)
    normed = (xloc * lax.rsqrt(jnp.mean(xloc * xloc, axis=-1, keepdims=True) + 1e-06)).astype(jnp.bfloat16)
    piece = lax.all_gather(normed, "cols", axis=0, tiled=True)

    w_head = lax.dynamic_index_in_dim(w_out, core, axis=0, keepdims=False)
    piece, w_head = lax.optimization_barrier((piece, w_head))
    w_mine = lax.all_gather(w_head, "cols")
    w_other = recv_from(w_mine, "core", 1)

    all_cols, row_count = piece.shape[0], piece.shape[1]

    def project_in(x, lo, hi):
        w = w_in[:, :, lo * hdim : hi * hdim].reshape(width, -1)
        out = jnp.dot(x.reshape(-1, width), w, preferred_element_type=jnp.float32)
        return out.reshape(all_cols, row_count, heads_here, hi - lo, hdim)

    pc = project_in(piece, 4, 6)
    fk = feature_map(pc[..., 0, :]).astype(jnp.bfloat16)
    vcol = pc[..., 1, :].astype(jnp.bfloat16)
    states = jnp.einsum("crhk,crhv->chkv", fk, vcol, preferred_element_type=jnp.float32)
    scale = hdim ** (-0.5)
    causal = (jnp.arange(row_count)[:, None] >= jnp.arange(row_count)[None, :]).astype(jnp.float32)

    def rest(x):
        pr = project_in(x, 0, 4)
        qrow = head_norm(pr[..., 0, :]).astype(jnp.bfloat16)
        krow = head_norm(pr[..., 1, :]).astype(jnp.bfloat16)
        vrow = pr[..., 2, :].astype(jnp.bfloat16)
        fq = feature_map(pr[..., 3, :]).astype(jnp.bfloat16)
        inner = jnp.einsum("cthd,cshd->chts", fq, fk, preferred_element_type=jnp.float32) * causal
        local = jnp.einsum("chts,cshv->cthv", inner, vcol.astype(jnp.float32), precision=high)
        return qrow, krow, vrow, fq, local

    def row_attention(qrow, krow, vrow, fq, local):
        score = jnp.einsum("crhd,erhd->rhce", qrow, krow, preferred_element_type=jnp.float32) * scale
        expo = jnp.exp(score)
        weights = (expo / jnp.sum(expo, axis=-1, keepdims=True)).astype(jnp.bfloat16)
        orow = jnp.einsum("rhce,erhd->crhd", weights, vrow, preferred_element_type=jnp.float32).astype(
            jnp.bfloat16
        )
        return orow, fq, local

    prior, (orow, fq, local) = exclusive_rows_scan(states, (piece,), rest, row_attention)

    carried = jnp.einsum("cthk,chkv->cthv", fq.astype(jnp.float32), prior, precision=high)
    ocol = head_norm(carried + local).astype(jnp.bfloat16)
    both = to_owners(jnp.concatenate([orow, ocol], axis=3))

    other_head = 1 - core

    def project(vals, w, head):
        v = lax.dynamic_index_in_dim(vals, head, axis=3, keepdims=False)
        return jnp.einsum("scrf,sfn->crn", v, w, preferred_element_type=jnp.float32)

    mixed = project(both, w_mine, core) + project(both, w_other, other_head)
    return mixed.astype(jnp.bfloat16)


def split_mesh(mesh):
    devs = mesh.devices
    n_rows, n_cols = devs.shape
    try:
        nx = len({d.coords[0] for d in devs.flat})
    except Exception:
        nx = 4
    ny = n_rows // (nx * 2)
    return Mesh(devs.reshape(ny, nx, 2, n_cols), ROWS_AXES + ("cols",))


def solution(mesh):
    m4 = split_mesh(mesh)
    spec = P("cols", ROWS_AXES, None)
    return jax.shard_map(
        body,
        mesh=m4,
        in_specs=(spec, P(None, "cols", None), P("cols", None, None)),
        out_specs=spec,
        check_vma=False,
    )
```

```python
import jax
import jax.numpy as jnp
import numpy as np
from jax import lax
from jax.sharding import Mesh, PartitionSpec as P

ROWS_AXES = ("y", "x", "core")


def head_norm(values):
    return values * lax.rsqrt(jnp.mean(values * values, axis=-1, keepdims=True) + 1e-06)


def feature_map(values):
    return jax.nn.elu(values) + 1.0


def recv_from(v, axis, k):
    n = lax.axis_size(axis)
    return lax.ppermute(v, axis, [(i, (i + k) % n) for i in range(n)])


def line_prefix(v, axis, held=None):
    n = lax.axis_size(axis)
    me = lax.axis_index(axis)
    sent = v.astype(jnp.bfloat16)
    got = [recv_from(sent, axis, k) for k in range(1, n)]
    got, held = lax.optimization_barrier((got, held))
    before = jnp.zeros_like(v)
    total = v
    for k, g in enumerate(got, start=1):
        g = g.astype(v.dtype)
        before = before + jnp.where(k <= me, g, jnp.zeros_like(g))
        total = total + g
    return before, total, held


def exclusive_rows_scan(states, inputs, x_work, y_work):
    core = lax.axis_index("core")
    other = recv_from(states, "core", 1)
    other, inputs = lax.optimization_barrier((other, inputs))
    xdone = x_work(*inputs)
    total = states + other
    own = jnp.where(core == 1, other, jnp.zeros_like(other))
    half = total.shape[0] // 2
    mine = lax.dynamic_slice_in_dim(total, core * half, half, axis=0)
    xpre, xsum, xdone = line_prefix(mine, "x", xdone)
    ydone = y_work(*xdone)
    ypre, _, ydone = line_prefix(xsum, "y", ydone)
    part = ypre + xpre
    part_other = recv_from(part, "core", 1)
    lo = jnp.where(core == 0, part, part_other)
    hi = jnp.where(core == 0, part_other, part)
    return jnp.concatenate([lo, hi], axis=0) + own, ydone


def to_owners(res):
    n = lax.axis_size("cols")
    g = lax.axis_index("cols")
    blocks = res.reshape(n, res.shape[0] // n, *res.shape[1:])
    out = [(g, lax.dynamic_index_in_dim(blocks, g, axis=0, keepdims=False))]
    for k in range(1, n):
        send = lax.dynamic_index_in_dim(blocks, (g + k) % n, axis=0, keepdims=False)
        out.append(((g - k) % n, recv_from(send, "cols", k)))
    return out


def body(sheet, w_in, w_out):
    high = lax.Precision.HIGHEST
    width = sheet.shape[2]
    heads_here = w_in.shape[1]
    hdim = w_out.shape[1] // 2
    core = lax.axis_index("core")

    xloc = sheet.astype(jnp.float32)
    normed = (xloc * lax.rsqrt(jnp.mean(xloc * xloc, axis=-1, keepdims=True) + 1e-06)).astype(jnp.bfloat16)
    piece = lax.all_gather(normed, "cols", axis=0, tiled=True)

    w_head = lax.dynamic_index_in_dim(w_out, core, axis=0, keepdims=False)
    piece, w_head = lax.optimization_barrier((piece, w_head))
    w_mine = lax.all_gather(w_head, "cols")
    w_other = recv_from(w_mine, "core", 1)

    all_cols, row_count = piece.shape[0], piece.shape[1]

    def project_in(x, lo, hi):
        w = w_in[:, :, lo * hdim : hi * hdim].reshape(width, -1)
        out = jnp.dot(x.reshape(-1, width), w, preferred_element_type=jnp.float32)
        return out.reshape(all_cols, row_count, heads_here, hi - lo, hdim)

    pc = project_in(piece, 4, 6)
    fk = feature_map(pc[..., 0, :]).astype(jnp.bfloat16)
    vcol = pc[..., 1, :].astype(jnp.bfloat16)
    states = jnp.einsum("crhk,crhv->chkv", fk, vcol, preferred_element_type=jnp.float32)
    scale = hdim ** (-0.5)
    causal = (jnp.arange(row_count)[:, None] >= jnp.arange(row_count)[None, :]).astype(jnp.float32)

    def rest(x):
        pr = project_in(x, 0, 4)
        qrow = head_norm(pr[..., 0, :]).astype(jnp.bfloat16)
        krow = head_norm(pr[..., 1, :]).astype(jnp.bfloat16)
        vrow = pr[..., 2, :].astype(jnp.bfloat16)
        fq = feature_map(pr[..., 3, :]).astype(jnp.bfloat16)
        inner = jnp.einsum("cthd,cshd->chts", fq, fk, preferred_element_type=jnp.float32) * causal
        local = jnp.einsum("chts,cshv->cthv", inner, vcol.astype(jnp.float32), precision=high)
        return qrow, krow, vrow, fq, local

    def row_attention(qrow, krow, vrow, fq, local):
        score = jnp.einsum("crhd,erhd->rhce", qrow, krow, preferred_element_type=jnp.float32) * scale
        expo = jnp.exp(score)
        weights = (expo / jnp.sum(expo, axis=-1, keepdims=True)).astype(jnp.bfloat16)
        orow = jnp.einsum("rhce,erhd->crhd", weights, vrow, preferred_element_type=jnp.float32).astype(
            jnp.bfloat16
        )
        return orow, fq, local

    prior, (orow, fq, local) = exclusive_rows_scan(states, (piece,), rest, row_attention)

    carried = jnp.einsum("cthk,chkv->cthv", fq.astype(jnp.float32), prior, precision=high)
    ocol = head_norm(carried + local).astype(jnp.bfloat16)
    both = to_owners(jnp.concatenate([orow, ocol], axis=3))

    lo = jnp.where(core == 0, w_mine, w_other)
    hi = jnp.where(core == 0, w_other, w_mine)
    w_pair = jnp.stack([lo, hi], axis=1)
    mixed = None
    for src_group, block in both:
        w = lax.dynamic_index_in_dim(w_pair, src_group, axis=0, keepdims=False)
        part = jnp.einsum("crhf,hfn->crn", block, w, preferred_element_type=jnp.float32)
        mixed = part if mixed is None else mixed + part
    return mixed.astype(jnp.bfloat16)


def split_mesh(mesh):
    devs = mesh.devices
    n_rows, n_cols = devs.shape
    try:
        nx = len({d.coords[0] for d in devs.flat})
    except Exception:
        nx = 4
    ny = n_rows // (nx * 2)
    return Mesh(devs.reshape(ny, nx, 2, n_cols), ROWS_AXES + ("cols",))


def solution(mesh):
    m4 = split_mesh(mesh)
    spec = P("cols", ROWS_AXES, None)
    return jax.shard_map(
        body,
        mesh=m4,
        in_specs=(spec, P(None, "cols", None), P("cols", None, None)),
        out_specs=spec,
        check_vma=False,
    )
```

```python
import jax
import jax.numpy as jnp
import numpy as np
from jax import lax
from jax.sharding import Mesh, PartitionSpec as P

ROWS_AXES = ("y", "x", "core")


def head_norm(values):
    return values * lax.rsqrt(jnp.mean(values * values, axis=-1, keepdims=True) + 1e-06)


def feature_map(values):
    return jax.nn.elu(values) + 1.0


def recv_from(v, axis, k):
    n = lax.axis_size(axis)
    return lax.ppermute(v, axis, [(i, (i + k) % n) for i in range(n)])


def line_prefix(v, axis, held=None):
    n = lax.axis_size(axis)
    me = lax.axis_index(axis)
    sent = v.astype(jnp.bfloat16)
    got = [recv_from(sent, axis, k) for k in range(1, n)]
    got, held = lax.optimization_barrier((got, held))
    before = jnp.zeros_like(v)
    total = v
    for k, g in enumerate(got, start=1):
        g = g.astype(v.dtype)
        before = before + jnp.where(k <= me, g, jnp.zeros_like(g))
        total = total + g
    return before, total, held


def exclusive_rows_scan(states, inputs, x_work, y_work):
    core = lax.axis_index("core")
    other = recv_from(states, "core", 1)
    other, inputs = lax.optimization_barrier((other, inputs))
    xdone = x_work(*inputs)
    total = states + other
    own = jnp.where(core == 1, other, jnp.zeros_like(other))
    half = total.shape[0] // 2
    mine = lax.dynamic_slice_in_dim(total, core * half, half, axis=0)
    xpre, xsum, xdone = line_prefix(mine, "x", xdone)
    ydone = y_work(*xdone)
    ypre, _, ydone = line_prefix(xsum, "y", ydone)
    part = ypre + xpre
    part_other = recv_from(part, "core", 1)
    lo = jnp.where(core == 0, part, part_other)
    hi = jnp.where(core == 0, part_other, part)
    return jnp.concatenate([lo, hi], axis=0) + own, ydone


def to_owners(res):
    n = lax.axis_size("cols")
    g = lax.axis_index("cols")
    blocks = res.reshape(n, res.shape[0] // n, *res.shape[1:])
    out = [(g, lax.dynamic_index_in_dim(blocks, g, axis=0, keepdims=False))]
    for k in range(1, n):
        send = lax.dynamic_index_in_dim(blocks, (g + k) % n, axis=0, keepdims=False)
        out.append(((g - k) % n, recv_from(send, "cols", k)))
    return out


def body(sheet, w_in, w_out):
    high = lax.Precision.HIGHEST
    width = sheet.shape[2]
    heads_here = w_in.shape[1]
    hdim = w_out.shape[1] // 2
    core = lax.axis_index("core")

    xloc = sheet.astype(jnp.float32)
    normed = (xloc * lax.rsqrt(jnp.mean(xloc * xloc, axis=-1, keepdims=True) + 1e-06)).astype(jnp.bfloat16)
    piece = lax.all_gather(normed, "cols", axis=0, tiled=True)

    w_head = lax.dynamic_index_in_dim(w_out, core, axis=0, keepdims=False)
    piece, w_head = lax.optimization_barrier((piece, w_head))
    w_mine = lax.all_gather(w_head, "cols")
    w_other = recv_from(w_mine, "core", 1)

    all_cols, row_count = piece.shape[0], piece.shape[1]

    def project_in(x, lo, hi):
        w = w_in[:, :, lo * hdim : hi * hdim].reshape(width, -1)
        out = jnp.dot(x.reshape(-1, width), w, preferred_element_type=jnp.float32)
        return out.reshape(all_cols, row_count, heads_here, hi - lo, hdim)

    pc = project_in(piece, 4, 6)
    fk = feature_map(pc[..., 0, :]).astype(jnp.bfloat16)
    vcol = pc[..., 1, :].astype(jnp.bfloat16)
    states = jnp.einsum("crhk,crhv->chkv", fk, vcol, preferred_element_type=jnp.float32)
    scale = hdim ** (-0.5)
    causal = (jnp.arange(row_count)[:, None] >= jnp.arange(row_count)[None, :]).astype(jnp.float32)

    def rest(x):
        pr = project_in(x, 0, 4)
        qrow = head_norm(pr[..., 0, :]).astype(jnp.bfloat16)
        krow = head_norm(pr[..., 1, :]).astype(jnp.bfloat16)
        vrow = pr[..., 2, :].astype(jnp.bfloat16)
        fq = feature_map(pr[..., 3, :]).astype(jnp.bfloat16)
        inner = jnp.einsum("cthd,cshd->chts", fq, fk, preferred_element_type=jnp.float32) * causal
        local = jnp.einsum("chts,cshv->cthv", inner, vcol.astype(jnp.float32), precision=high)
        return qrow, krow, vrow, fq, local

    def row_attention(qrow, krow, vrow, fq, local):
        q32, k32, v32 = (t.astype(jnp.float32) for t in (qrow, krow, vrow))
        score = jnp.sum(q32[:, None] * k32[None], axis=-1) * scale
        expo = jnp.exp(score)
        weights = (expo / jnp.sum(expo, axis=1, keepdims=True)).astype(jnp.bfloat16)
        orow = jnp.sum(weights.astype(jnp.float32)[..., None] * v32[None], axis=1).astype(jnp.bfloat16)
        return orow, fq, local

    prior, (orow, fq, local) = exclusive_rows_scan(states, (piece,), rest, row_attention)

    carried = jnp.einsum("cthk,chkv->cthv", fq.astype(jnp.float32), prior, precision=high)
    ocol = head_norm(carried + local).astype(jnp.bfloat16)
    both = to_owners(jnp.concatenate([orow, ocol], axis=3))

    mixed = None
    for src_group, block in both:
        for w_all, head in ((w_mine, core), (w_other, 1 - core)):
            w = lax.dynamic_index_in_dim(w_all, src_group, axis=0, keepdims=False)
            b = lax.dynamic_index_in_dim(block, head, axis=2, keepdims=False)
            part = jnp.einsum("crf,fn->crn", b, w, preferred_element_type=jnp.float32)
            mixed = part if mixed is None else mixed + part
    return mixed.astype(jnp.bfloat16)


def split_mesh(mesh):
    devs = mesh.devices
    n_rows, n_cols = devs.shape
    try:
        nx = len({d.coords[0] for d in devs.flat})
    except Exception:
        nx = 4
    ny = n_rows // (nx * 2)
    return Mesh(devs.reshape(ny, nx, 2, n_cols), ROWS_AXES + ("cols",))


def solution(mesh):
    m4 = split_mesh(mesh)
    spec = P("cols", ROWS_AXES, None)
    return jax.shard_map(
        body,
        mesh=m4,
        in_specs=(spec, P(None, "cols", None), P("cols", None, None)),
        out_specs=spec,
        check_vma=False,
    )
```

```python
import jax
import jax.numpy as jnp
import numpy as np
from jax import lax
from jax.sharding import Mesh, PartitionSpec as P

ROWS_AXES = ("y", "x", "core")


def head_norm(values):
    return values * lax.rsqrt(jnp.mean(values * values, axis=-1, keepdims=True) + 1e-06)


def feature_map(values):
    return jax.nn.elu(values) + 1.0


def recv_from(v, axis, k):
    n = lax.axis_size(axis)
    return lax.ppermute(v, axis, [(i, (i + k) % n) for i in range(n)])


def line_prefix(v, axis, held=None):
    n = lax.axis_size(axis)
    me = lax.axis_index(axis)
    sent = v.astype(jnp.bfloat16)
    got = [recv_from(sent, axis, k) for k in range(1, n)]
    got, held = lax.optimization_barrier((got, held))
    before = jnp.zeros_like(v)
    total = v
    for k, g in enumerate(got, start=1):
        g = g.astype(v.dtype)
        before = before + jnp.where(k <= me, g, jnp.zeros_like(g))
        total = total + g
    return before, total, held


def exclusive_rows_scan(states, inputs, x_work, y_work):
    core = lax.axis_index("core")
    other = recv_from(states, "core", 1)
    other, inputs = lax.optimization_barrier((other, inputs))
    xdone = x_work(*inputs)
    total = states + other
    own = jnp.where(core == 1, other, jnp.zeros_like(other))
    half = total.shape[0] // 2
    mine = lax.dynamic_slice_in_dim(total, core * half, half, axis=0)
    xpre, xsum, xdone = line_prefix(mine, "x", xdone)
    ydone = y_work(*xdone)
    ypre, _, ydone = line_prefix(xsum, "y", ydone)
    part = ypre + xpre
    part_other = recv_from(part, "core", 1)
    lo = jnp.where(core == 0, part, part_other)
    hi = jnp.where(core == 0, part_other, part)
    return jnp.concatenate([lo, hi], axis=0) + own, ydone


def to_owners(res):
    n = lax.axis_size("cols")
    g = lax.axis_index("cols")
    blocks = res.reshape(n, res.shape[0] // n, *res.shape[1:])
    out = [(g, lax.dynamic_index_in_dim(blocks, g, axis=0, keepdims=False))]
    for k in range(1, n):
        send = lax.dynamic_index_in_dim(blocks, (g + k) % n, axis=0, keepdims=False)
        out.append(((g - k) % n, recv_from(send, "cols", k)))
    return out


def body(sheet, w_in, w_out):
    high = lax.Precision.HIGHEST
    width = sheet.shape[2]
    heads_here = w_in.shape[1]
    hdim = w_out.shape[1] // 2
    core = lax.axis_index("core")

    xloc = sheet.astype(jnp.float32)
    normed = (xloc * lax.rsqrt(jnp.mean(xloc * xloc, axis=-1, keepdims=True) + 1e-06)).astype(jnp.bfloat16)
    piece = lax.all_gather(normed, "cols", axis=0, tiled=True)

    w_head = lax.dynamic_index_in_dim(w_out, core, axis=0, keepdims=False)
    piece, w_head = lax.optimization_barrier((piece, w_head))
    w_mine = lax.all_gather(w_head, "cols")
    w_other = recv_from(w_mine, "core", 1)

    all_cols, row_count = piece.shape[0], piece.shape[1]

    def project_in(x, lo, hi):
        w = w_in[:, :, lo * hdim : hi * hdim].reshape(width, -1)
        out = jnp.dot(x.reshape(-1, width), w, preferred_element_type=jnp.float32)
        return out.reshape(all_cols, row_count, heads_here, hi - lo, hdim)

    pc = project_in(piece, 4, 6)
    fk = feature_map(pc[..., 0, :]).astype(jnp.bfloat16)
    vcol = pc[..., 1, :].astype(jnp.bfloat16)
    states = jnp.einsum("crhk,crhv->chkv", fk, vcol, preferred_element_type=jnp.float32)
    scale = hdim ** (-0.5)
    causal = (jnp.arange(row_count)[:, None] >= jnp.arange(row_count)[None, :]).astype(jnp.float32)

    def rest(x):
        pr = project_in(x, 0, 4)
        qrow = head_norm(pr[..., 0, :]).astype(jnp.bfloat16)
        krow = head_norm(pr[..., 1, :]).astype(jnp.bfloat16)
        vrow = pr[..., 2, :].astype(jnp.bfloat16)
        fq = feature_map(pr[..., 3, :]).astype(jnp.bfloat16)
        inner = jnp.einsum("cthd,cshd->chts", fq, fk, preferred_element_type=jnp.float32) * causal
        local = jnp.einsum("chts,cshv->cthv", inner, vcol.astype(jnp.float32), precision=high)
        return qrow, krow, vrow, fq, local

    def row_attention(qrow, krow, vrow, fq, local):
        q32, k32, v32 = (t.astype(jnp.float32) for t in (qrow, krow, vrow))
        score = jnp.sum(q32[:, None] * k32[None], axis=-1) * scale
        expo = jnp.exp(score)
        weights = (expo / jnp.sum(expo, axis=1, keepdims=True)).astype(jnp.bfloat16)
        orow = jnp.sum(weights.astype(jnp.float32)[..., None] * v32[None], axis=1).astype(jnp.bfloat16)
        return orow, fq, local

    prior, (orow, fq, local) = exclusive_rows_scan(states, (piece,), rest, row_attention)

    carried = jnp.einsum("cthk,chkv->cthv", fq.astype(jnp.float32), prior, precision=high)
    ocol = head_norm(carried + local).astype(jnp.bfloat16)
    ocol, w_other = lax.optimization_barrier((ocol, w_other))
    both = to_owners(jnp.concatenate([orow, ocol], axis=3))

    heads_order = jnp.stack([core, 1 - core])
    mixed = None
    for src_group, block in both:
        w = jnp.stack(
            [lax.dynamic_index_in_dim(w_all, src_group, axis=0, keepdims=False) for w_all in (w_mine, w_other)]
        )
        b = jnp.take(block, heads_order, axis=2)
        part = jnp.einsum("crhf,hfn->crn", b, w, preferred_element_type=jnp.float32)
        mixed = part if mixed is None else mixed + part
    return mixed.astype(jnp.bfloat16)


def split_mesh(mesh):
    devs = mesh.devices
    n_rows, n_cols = devs.shape
    try:
        nx = len({d.coords[0] for d in devs.flat})
    except Exception:
        nx = 4
    ny = n_rows // (nx * 2)
    return Mesh(devs.reshape(ny, nx, 2, n_cols), ROWS_AXES + ("cols",))


def solution(mesh):
    m4 = split_mesh(mesh)
    spec = P("cols", ROWS_AXES, None)
    return jax.shard_map(
        body,
        mesh=m4,
        in_specs=(spec, P(None, "cols", None), P("cols", None, None)),
        out_specs=spec,
        check_vma=False,
    )
```

```python
import jax
import jax.numpy as jnp
import numpy as np
from jax import lax
from jax.sharding import Mesh, PartitionSpec as P

ROWS_AXES = ("y", "x", "core")


def head_norm(values):
    return values * lax.rsqrt(jnp.mean(values * values, axis=-1, keepdims=True) + 1e-06)


def feature_map(values):
    return jax.nn.elu(values) + 1.0


def recv_from(v, axis, k):
    n = lax.axis_size(axis)
    return lax.ppermute(v, axis, [(i, (i + k) % n) for i in range(n)])


def line_prefix(v, axis, held=None):
    n = lax.axis_size(axis)
    me = lax.axis_index(axis)
    sent = v.astype(jnp.bfloat16)
    got = [recv_from(sent, axis, k) for k in range(1, n)]
    got, held = lax.optimization_barrier((got, held))
    before = jnp.zeros_like(v)
    total = v
    for k, g in enumerate(got, start=1):
        g = g.astype(v.dtype)
        before = before + jnp.where(k <= me, g, jnp.zeros_like(g))
        total = total + g
    return before, total, held


def exclusive_rows_scan(states, inputs, x_work, y_work):
    core = lax.axis_index("core")
    other = recv_from(states, "core", 1)
    other, inputs = lax.optimization_barrier((other, inputs))
    xdone = x_work(*inputs)
    total = states + other
    own = jnp.where(core == 1, other, jnp.zeros_like(other))
    half = total.shape[0] // 2
    mine = lax.dynamic_slice_in_dim(total, core * half, half, axis=0)
    xpre, xsum, xdone = line_prefix(mine, "x", xdone)
    ydone = y_work(*xdone)
    ypre, _, ydone = line_prefix(xsum, "y", ydone)
    part = ypre + xpre
    part_other = recv_from(part, "core", 1)
    lo = jnp.where(core == 0, part, part_other)
    hi = jnp.where(core == 0, part_other, part)
    return jnp.concatenate([lo, hi], axis=0) + own, ydone


def to_owners(res):
    n = lax.axis_size("cols")
    g = lax.axis_index("cols")
    blocks = res.reshape(n, res.shape[0] // n, *res.shape[1:])
    out = [(g, lax.dynamic_index_in_dim(blocks, g, axis=0, keepdims=False))]
    for k in range(1, n):
        send = lax.dynamic_index_in_dim(blocks, (g + k) % n, axis=0, keepdims=False)
        out.append(((g - k) % n, recv_from(send, "cols", k)))
    return out


def body(sheet, w_in, w_out):
    high = lax.Precision.HIGHEST
    width = sheet.shape[2]
    heads_here = w_in.shape[1]
    hdim = w_out.shape[1] // 2
    core = lax.axis_index("core")

    xloc = sheet.astype(jnp.float32)
    normed = (xloc * lax.rsqrt(jnp.mean(xloc * xloc, axis=-1, keepdims=True) + 1e-06)).astype(jnp.bfloat16)
    piece = lax.all_gather(normed, "cols", axis=0, tiled=True)

    w_head = lax.dynamic_index_in_dim(w_out, core, axis=0, keepdims=False)
    piece, w_head = lax.optimization_barrier((piece, w_head))
    w_mine = lax.all_gather(w_head, "cols")
    w_other = recv_from(w_mine, "core", 1)

    all_cols, row_count = piece.shape[0], piece.shape[1]

    def project_in(x, lo, hi):
        w = w_in[:, :, lo * hdim : hi * hdim].reshape(width, -1)
        out = jnp.dot(x.reshape(-1, width), w, preferred_element_type=jnp.float32)
        return out.reshape(all_cols, row_count, heads_here, hi - lo, hdim)

    pc = project_in(piece, 4, 6)
    fk = feature_map(pc[..., 0, :]).astype(jnp.bfloat16)
    vcol = pc[..., 1, :].astype(jnp.bfloat16)
    states = jnp.einsum("crhk,crhv->chkv", fk, vcol, preferred_element_type=jnp.float32)
    scale = hdim ** (-0.5)
    causal = (jnp.arange(row_count)[:, None] >= jnp.arange(row_count)[None, :]).astype(jnp.float32)

    def rest(x):
        pr = project_in(x, 0, 4)
        qrow = head_norm(pr[..., 0, :]).astype(jnp.bfloat16)
        krow = head_norm(pr[..., 1, :]).astype(jnp.bfloat16)
        vrow = pr[..., 2, :].astype(jnp.bfloat16)
        fq = feature_map(pr[..., 3, :]).astype(jnp.bfloat16)
        inner = jnp.einsum("cthd,cshd->chts", fq, fk, preferred_element_type=jnp.float32) * causal
        local = jnp.einsum("chts,cshv->cthv", inner, vcol.astype(jnp.float32), precision=high)
        return qrow, krow, vrow, fq, local

    def row_attention(qrow, krow, vrow, fq, local):
        q32, k32, v32 = (t.astype(jnp.float32) for t in (qrow, krow, vrow))
        score = jnp.sum(q32[:, None] * k32[None], axis=-1) * scale
        expo = jnp.exp(score)
        weights = (expo / jnp.sum(expo, axis=1, keepdims=True)).astype(jnp.bfloat16)
        orow = jnp.sum(weights.astype(jnp.float32)[..., None] * v32[None], axis=1).astype(jnp.bfloat16)
        return orow, fq, local

    prior, (orow, fq, local) = exclusive_rows_scan(states, (piece,), rest, row_attention)

    carried = jnp.einsum("cthk,chkv->cthv", fq.astype(jnp.float32), prior, precision=high)
    ocol = head_norm(carried + local).astype(jnp.bfloat16)
    w_pair = jnp.stack([w_mine, w_other], axis=1)
    ocol, w_pair = lax.optimization_barrier((ocol, w_pair))
    both = to_owners(jnp.concatenate([orow, ocol], axis=3))

    mixed = None
    for src_group, block in both:
        w = lax.dynamic_index_in_dim(w_pair, src_group, axis=0, keepdims=False)
        b = jnp.where(core == 0, block, block[:, :, ::-1])
        part = jnp.einsum("crhf,hfn->crn", b, w, preferred_element_type=jnp.float32)
        mixed = part if mixed is None else mixed + part
    return mixed.astype(jnp.bfloat16)


def split_mesh(mesh):
    devs = mesh.devices
    n_rows, n_cols = devs.shape
    try:
        nx = len({d.coords[0] for d in devs.flat})
    except Exception:
        nx = 4
    ny = n_rows // (nx * 2)
    return Mesh(devs.reshape(ny, nx, 2, n_cols), ROWS_AXES + ("cols",))


def solution(mesh):
    m4 = split_mesh(mesh)
    spec = P("cols", ROWS_AXES, None)
    return jax.shard_map(
        body,
        mesh=m4,
        in_specs=(spec, P(None, "cols", None), P("cols", None, None)),
        out_specs=spec,
        check_vma=False,
    )
```

```python
import jax
import jax.numpy as jnp
import numpy as np
from jax import lax
from jax.sharding import Mesh, PartitionSpec as P

ROWS_AXES = ("y", "x", "core")


def head_norm(values):
    return values * lax.rsqrt(jnp.mean(values * values, axis=-1, keepdims=True) + 1e-06)


def feature_map(values):
    return jax.nn.elu(values) + 1.0


def recv_from(v, axis, k):
    n = lax.axis_size(axis)
    return lax.ppermute(v, axis, [(i, (i + k) % n) for i in range(n)])


def line_prefix(v, axis, held=None):
    n = lax.axis_size(axis)
    me = lax.axis_index(axis)
    sent = v.astype(jnp.bfloat16)
    got = [recv_from(sent, axis, k) for k in range(1, n)]
    got, held = lax.optimization_barrier((got, held))
    before = jnp.zeros_like(v)
    total = v
    for k, g in enumerate(got, start=1):
        g = g.astype(v.dtype)
        before = before + jnp.where(k <= me, g, jnp.zeros_like(g))
        total = total + g
    return before, total, held


def exclusive_rows_scan(states, inputs, x_work, y_work):
    core = lax.axis_index("core")
    other = recv_from(states, "core", 1)
    other, inputs = lax.optimization_barrier((other, inputs))
    xdone = x_work(*inputs)
    total = states + other
    own = jnp.where(core == 1, other, jnp.zeros_like(other))
    half = total.shape[0] // 2
    mine = lax.dynamic_slice_in_dim(total, core * half, half, axis=0)
    xpre, xsum, xdone = line_prefix(mine, "x", xdone)
    ydone = y_work(*xdone)
    ypre, _, ydone = line_prefix(xsum, "y", ydone)
    part = ypre + xpre
    part_other = recv_from(part, "core", 1)
    lo = jnp.where(core == 0, part, part_other)
    hi = jnp.where(core == 0, part_other, part)
    return jnp.concatenate([lo, hi], axis=0) + own, ydone


def to_owners(res):
    n = lax.axis_size("cols")
    g = lax.axis_index("cols")
    blocks = res.reshape(n, res.shape[0] // n, *res.shape[1:])
    out = [(g, lax.dynamic_index_in_dim(blocks, g, axis=0, keepdims=False))]
    for k in range(1, n):
        send = lax.dynamic_index_in_dim(blocks, (g + k) % n, axis=0, keepdims=False)
        out.append(((g - k) % n, recv_from(send, "cols", k)))
    return out


def body(sheet, w_in, w_out):
    high = lax.Precision.HIGHEST
    width = sheet.shape[2]
    heads_here = w_in.shape[1]
    hdim = w_out.shape[1] // 2
    core = lax.axis_index("core")

    xloc = sheet.astype(jnp.float32)
    normed = (xloc * lax.rsqrt(jnp.mean(xloc * xloc, axis=-1, keepdims=True) + 1e-06)).astype(jnp.bfloat16)
    piece = lax.all_gather(normed, "cols", axis=0, tiled=True)

    piece, w_held = lax.optimization_barrier((piece, w_out))
    w_pair = lax.all_gather(w_held, "cols")

    all_cols, row_count = piece.shape[0], piece.shape[1]

    def project_in(x, lo, hi):
        w = w_in[:, :, lo * hdim : hi * hdim].reshape(width, -1)
        out = jnp.dot(x.reshape(-1, width), w, preferred_element_type=jnp.float32)
        return out.reshape(all_cols, row_count, heads_here, hi - lo, hdim)

    pc = project_in(piece, 4, 6)
    fk = feature_map(pc[..., 0, :]).astype(jnp.bfloat16)
    vcol = pc[..., 1, :].astype(jnp.bfloat16)
    states = jnp.einsum("crhk,crhv->chkv", fk, vcol, preferred_element_type=jnp.float32)
    scale = hdim ** (-0.5)
    causal = (jnp.arange(row_count)[:, None] >= jnp.arange(row_count)[None, :]).astype(jnp.float32)

    def rest(x):
        pr = project_in(x, 0, 4)
        qrow = head_norm(pr[..., 0, :]).astype(jnp.bfloat16)
        krow = head_norm(pr[..., 1, :]).astype(jnp.bfloat16)
        vrow = pr[..., 2, :].astype(jnp.bfloat16)
        fq = feature_map(pr[..., 3, :]).astype(jnp.bfloat16)
        inner = jnp.einsum("cthd,cshd->chts", fq, fk, preferred_element_type=jnp.float32) * causal
        local = jnp.einsum("chts,cshv->cthv", inner, vcol.astype(jnp.float32), precision=high)
        return qrow, krow, vrow, fq, local

    def row_attention(qrow, krow, vrow, fq, local):
        q32, k32, v32 = (t.astype(jnp.float32) for t in (qrow, krow, vrow))
        score = jnp.sum(q32[:, None] * k32[None], axis=-1) * scale
        expo = jnp.exp(score)
        weights = (expo / jnp.sum(expo, axis=1, keepdims=True)).astype(jnp.bfloat16)
        orow = jnp.sum(weights.astype(jnp.float32)[..., None] * v32[None], axis=1).astype(jnp.bfloat16)
        return orow, fq, local

    prior, (orow, fq, local) = exclusive_rows_scan(states, (piece,), rest, row_attention)

    carried = jnp.einsum("cthk,chkv->cthv", fq.astype(jnp.float32), prior, precision=high)
    ocol = head_norm(carried + local).astype(jnp.bfloat16)
    both = to_owners(jnp.concatenate([orow, ocol], axis=3))

    mixed = None
    for src_group, block in both:
        w = lax.dynamic_index_in_dim(w_pair, src_group, axis=0, keepdims=False)
        part = jnp.einsum("crhf,hfn->crn", block, w, preferred_element_type=jnp.float32)
        mixed = part if mixed is None else mixed + part
    return mixed.astype(jnp.bfloat16)


def split_mesh(mesh):
    devs = mesh.devices
    n_rows, n_cols = devs.shape
    try:
        nx = len({d.coords[0] for d in devs.flat})
    except Exception:
        nx = 4
    ny = n_rows // (nx * 2)
    return Mesh(devs.reshape(ny, nx, 2, n_cols), ROWS_AXES + ("cols",))


def solution(mesh):
    m4 = split_mesh(mesh)
    spec = P("cols", ROWS_AXES, None)
    return jax.shard_map(
        body,
        mesh=m4,
        in_specs=(spec, P(None, "cols", None), P("cols", None, None)),
        out_specs=spec,
        check_vma=False,
    )
```

```python
import jax
import jax.numpy as jnp
import numpy as np
from jax import lax
from jax.sharding import Mesh, PartitionSpec as P

ROWS_AXES = ("y", "x", "core")


def head_norm(values):
    return values * lax.rsqrt(jnp.mean(values * values, axis=-1, keepdims=True) + 1e-06)


def feature_map(values):
    return jax.nn.elu(values) + 1.0


def recv_from(v, axis, k):
    n = lax.axis_size(axis)
    return lax.ppermute(v, axis, [(i, (i + k) % n) for i in range(n)])


def line_prefix(v, axis, held=None):
    n = lax.axis_size(axis)
    me = lax.axis_index(axis)
    sent = v.astype(jnp.bfloat16)
    got = [recv_from(sent, axis, k) for k in range(1, n)]
    got, held = lax.optimization_barrier((got, held))
    before = jnp.zeros_like(v)
    total = v
    for k, g in enumerate(got, start=1):
        g = g.astype(v.dtype)
        before = before + jnp.where(k <= me, g, jnp.zeros_like(g))
        total = total + g
    return before, total, held


def exclusive_rows_scan(states, inputs, x_work, y_work):
    core = lax.axis_index("core")
    other = recv_from(states, "core", 1)
    other, inputs = lax.optimization_barrier((other, inputs))
    xdone = x_work(*inputs)
    total = states + other
    own = jnp.where(core == 1, other, jnp.zeros_like(other))
    half = total.shape[0] // 2
    mine = lax.dynamic_slice_in_dim(total, core * half, half, axis=0)
    xpre, xsum, xdone = line_prefix(mine, "x", xdone)
    ydone = y_work(*xdone)
    ypre, _, ydone = line_prefix(xsum, "y", ydone)
    part = ypre + xpre
    part_other = recv_from(part, "core", 1)
    lo = jnp.where(core == 0, part, part_other)
    hi = jnp.where(core == 0, part_other, part)
    return jnp.concatenate([lo, hi], axis=0) + own, ydone


def to_owners(res):
    n = lax.axis_size("cols")
    g = lax.axis_index("cols")
    blocks = res.reshape(n, res.shape[0] // n, *res.shape[1:])
    out = [(g, lax.dynamic_index_in_dim(blocks, g, axis=0, keepdims=False))]
    for k in range(1, n):
        send = lax.dynamic_index_in_dim(blocks, (g + k) % n, axis=0, keepdims=False)
        out.append(((g - k) % n, recv_from(send, "cols", k)))
    return out


def body(sheet, w_in, w_out):
    high = lax.Precision.HIGHEST
    width = sheet.shape[2]
    heads_here = w_in.shape[1]
    hdim = w_out.shape[1] // 2
    core = lax.axis_index("core")

    xloc = sheet.astype(jnp.float32)
    normed = (xloc * lax.rsqrt(jnp.mean(xloc * xloc, axis=-1, keepdims=True) + 1e-06)).astype(jnp.bfloat16)
    half_rows = normed.shape[1] // 2
    piece = jnp.concatenate(
        [
            lax.all_gather(normed[:, :half_rows], "cols", axis=0, tiled=True),
            lax.all_gather(normed[:, half_rows:], "cols", axis=0, tiled=True),
        ],
        axis=1,
    )

    piece, w_held = lax.optimization_barrier((piece, w_out))
    w_pair = lax.all_gather(w_held, "cols")

    all_cols, row_count = piece.shape[0], piece.shape[1]

    def project_in(x, lo, hi):
        w = w_in[:, :, lo * hdim : hi * hdim].reshape(width, -1)
        out = jnp.dot(x.reshape(-1, width), w, preferred_element_type=jnp.float32)
        return out.reshape(all_cols, row_count, heads_here, hi - lo, hdim)

    pc = project_in(piece, 4, 6)
    fk = feature_map(pc[..., 0, :]).astype(jnp.bfloat16)
    vcol = pc[..., 1, :].astype(jnp.bfloat16)
    states = jnp.einsum("crhk,crhv->chkv", fk, vcol, preferred_element_type=jnp.float32)
    scale = hdim ** (-0.5)
    causal = (jnp.arange(row_count)[:, None] >= jnp.arange(row_count)[None, :]).astype(jnp.float32)

    def rest(x):
        pr = project_in(x, 0, 4)
        qrow = head_norm(pr[..., 0, :]).astype(jnp.bfloat16)
        krow = head_norm(pr[..., 1, :]).astype(jnp.bfloat16)
        vrow = pr[..., 2, :].astype(jnp.bfloat16)
        fq = feature_map(pr[..., 3, :]).astype(jnp.bfloat16)
        inner = jnp.einsum("cthd,cshd->chts", fq, fk, preferred_element_type=jnp.float32) * causal
        local = jnp.einsum("chts,cshv->cthv", inner, vcol.astype(jnp.float32), precision=high)
        return qrow, krow, vrow, fq, local

    def row_attention(qrow, krow, vrow, fq, local):
        q32, k32, v32 = (t.astype(jnp.float32) for t in (qrow, krow, vrow))
        score = jnp.sum(q32[:, None] * k32[None], axis=-1) * scale
        expo = jnp.exp(score)
        weights = (expo / jnp.sum(expo, axis=1, keepdims=True)).astype(jnp.bfloat16)
        orow = jnp.sum(weights.astype(jnp.float32)[..., None] * v32[None], axis=1).astype(jnp.bfloat16)
        return orow, fq, local

    prior, (orow, fq, local) = exclusive_rows_scan(states, (piece,), rest, row_attention)

    carried = jnp.einsum("cthk,chkv->cthv", fq.astype(jnp.float32), prior, precision=high)
    ocol = head_norm(carried + local).astype(jnp.bfloat16)
    both = to_owners(jnp.concatenate([orow, ocol], axis=3))

    mixed = None
    for src_group, block in both:
        w = lax.dynamic_index_in_dim(w_pair, src_group, axis=0, keepdims=False)
        part = jnp.einsum("crhf,hfn->crn", block, w, preferred_element_type=jnp.float32)
        mixed = part if mixed is None else mixed + part
    return mixed.astype(jnp.bfloat16)


def split_mesh(mesh):
    devs = mesh.devices
    n_rows, n_cols = devs.shape
    try:
        nx = len({d.coords[0] for d in devs.flat})
    except Exception:
        nx = 4
    ny = n_rows // (nx * 2)
    return Mesh(devs.reshape(ny, nx, 2, n_cols), ROWS_AXES + ("cols",))


def solution(mesh):
    m4 = split_mesh(mesh)
    spec = P("cols", ROWS_AXES, None)
    return jax.shard_map(
        body,
        mesh=m4,
        in_specs=(spec, P(None, "cols", None), P("cols", None, None)),
        out_specs=spec,
        check_vma=False,
    )
```

```python
import jax
import jax.numpy as jnp
import numpy as np
from jax import lax
from jax.sharding import Mesh, PartitionSpec as P

ROWS_AXES = ("y", "x", "core")


def head_norm(values):
    return values * lax.rsqrt(jnp.mean(values * values, axis=-1, keepdims=True) + 1e-06)


def feature_map(values):
    return jax.nn.elu(values) + 1.0


def recv_from(v, axis, k):
    n = lax.axis_size(axis)
    return lax.ppermute(v, axis, [(i, (i + k) % n) for i in range(n)])


def line_prefix(v, axis, held=None):
    n = lax.axis_size(axis)
    me = lax.axis_index(axis)
    sent = v.astype(jnp.bfloat16)
    got = [recv_from(sent, axis, k) for k in range(1, n)]
    got, held = lax.optimization_barrier((got, held))
    before = jnp.zeros_like(v)
    total = v
    for k, g in enumerate(got, start=1):
        g = g.astype(v.dtype)
        before = before + jnp.where(k <= me, g, jnp.zeros_like(g))
        total = total + g
    return before, total, held


def exclusive_rows_scan(states, inputs, x_work, y_work):
    core = lax.axis_index("core")
    other = recv_from(states, "core", 1)
    other, inputs = lax.optimization_barrier((other, inputs))
    xdone = x_work(*inputs)
    total = states + other
    own = jnp.where(core == 1, other, jnp.zeros_like(other))
    half = total.shape[0] // 2
    mine = lax.dynamic_slice_in_dim(total, core * half, half, axis=0)
    xpre, xsum, xdone = line_prefix(mine, "x", xdone)
    ydone = y_work(*xdone)
    ypre, _, ydone = line_prefix(xsum, "y", ydone)
    part = ypre + xpre
    part_other = recv_from(part, "core", 1)
    lo = jnp.where(core == 0, part, part_other)
    hi = jnp.where(core == 0, part_other, part)
    return jnp.concatenate([lo, hi], axis=0) + own, ydone


def ring_gather(x, axis):
    n = lax.axis_size(axis)
    fwd = bwd = x
    got = {0: x}
    for s in range(1, (n + 1) // 2):
        fwd = recv_from(fwd, axis, 1)
        bwd = recv_from(bwd, axis, n - 1)
        got[n - s] = fwd
        got[s] = bwd
    if n % 2 == 0 and n > 1:
        h = x.shape[1] // 2
        a = recv_from(fwd[:, :h], axis, 1)
        b = recv_from(bwd[:, h:], axis, n - 1)
        got[n // 2] = jnp.concatenate([a, b], axis=1)
    return jnp.concatenate([got[d] for d in range(n)], axis=0)


def to_owners(res):
    n = lax.axis_size("cols")
    g = lax.axis_index("cols")
    blocks = res.reshape(n, res.shape[0] // n, *res.shape[1:])
    out = [(g, blocks[0])]
    for k in range(1, n):
        out.append(((g - k) % n, recv_from(blocks[k], "cols", k)))
    return out


def body(sheet, w_in, w_out):
    high = lax.Precision.HIGHEST
    width = sheet.shape[2]
    heads_here = w_in.shape[1]
    hdim = w_out.shape[1] // 2
    core = lax.axis_index("core")

    xloc = sheet.astype(jnp.float32)
    normed = (xloc * lax.rsqrt(jnp.mean(xloc * xloc, axis=-1, keepdims=True) + 1e-06)).astype(jnp.bfloat16)
    piece = ring_gather(normed, "cols")

    piece, w_held = lax.optimization_barrier((piece, w_out))
    w_pair = lax.all_gather(w_held, "cols")

    all_cols, row_count = piece.shape[0], piece.shape[1]

    def project_in(x, lo, hi):
        w = w_in[:, :, lo * hdim : hi * hdim].reshape(width, -1)
        out = jnp.dot(x.reshape(-1, width), w, preferred_element_type=jnp.float32)
        return out.reshape(all_cols, row_count, heads_here, hi - lo, hdim)

    pc = project_in(piece, 4, 6)
    fk = feature_map(pc[..., 0, :]).astype(jnp.bfloat16)
    vcol = pc[..., 1, :].astype(jnp.bfloat16)
    states = jnp.einsum("crhk,crhv->chkv", fk, vcol, preferred_element_type=jnp.float32)
    scale = hdim ** (-0.5)
    causal = (jnp.arange(row_count)[:, None] >= jnp.arange(row_count)[None, :]).astype(jnp.float32)

    def rest(x):
        pr = project_in(x, 0, 4)
        qrow = head_norm(pr[..., 0, :]).astype(jnp.bfloat16)
        krow = head_norm(pr[..., 1, :]).astype(jnp.bfloat16)
        vrow = pr[..., 2, :].astype(jnp.bfloat16)
        fq = feature_map(pr[..., 3, :]).astype(jnp.bfloat16)
        inner = jnp.einsum("cthd,cshd->chts", fq, fk, preferred_element_type=jnp.float32) * causal
        local = jnp.einsum("chts,cshv->cthv", inner, vcol.astype(jnp.float32), precision=high)
        return qrow, krow, vrow, fq, local

    def row_attention(qrow, krow, vrow, fq, local):
        q32, k32, v32 = (t.astype(jnp.float32) for t in (qrow, krow, vrow))
        score = jnp.sum(q32[:, None] * k32[None], axis=-1) * scale
        expo = jnp.exp(score)
        weights = (expo / jnp.sum(expo, axis=1, keepdims=True)).astype(jnp.bfloat16)
        orow = jnp.sum(weights.astype(jnp.float32)[..., None] * v32[None], axis=1).astype(jnp.bfloat16)
        return orow, fq, local

    prior, (orow, fq, local) = exclusive_rows_scan(states, (piece,), rest, row_attention)

    carried = jnp.einsum("cthk,chkv->cthv", fq.astype(jnp.float32), prior, precision=high)
    ocol = head_norm(carried + local).astype(jnp.bfloat16)
    both = to_owners(jnp.concatenate([orow, ocol], axis=3))

    mixed = None
    for src_group, block in both:
        w = lax.dynamic_index_in_dim(w_pair, src_group, axis=0, keepdims=False)
        part = jnp.einsum("crhf,hfn->crn", block, w, preferred_element_type=jnp.float32)
        mixed = part if mixed is None else mixed + part
    return mixed.astype(jnp.bfloat16)


def split_mesh(mesh):
    devs = mesh.devices
    n_rows, n_cols = devs.shape
    try:
        nx = len({d.coords[0] for d in devs.flat})
    except Exception:
        nx = 4
    ny = n_rows // (nx * 2)
    return Mesh(devs.reshape(ny, nx, 2, n_cols), ROWS_AXES + ("cols",))


def solution(mesh):
    m4 = split_mesh(mesh)
    spec = P("cols", ROWS_AXES, None)
    return jax.shard_map(
        body,
        mesh=m4,
        in_specs=(spec, P(None, "cols", None), P("cols", None, None)),
        out_specs=spec,
        check_vma=False,
    )
```

```python
import jax
import jax.numpy as jnp
import numpy as np
from jax import lax
from jax.sharding import Mesh, PartitionSpec as P

ROWS_AXES = ("y", "x", "core")


def head_norm(values):
    return values * lax.rsqrt(jnp.mean(values * values, axis=-1, keepdims=True) + 1e-06)


def feature_map(values):
    return jax.nn.elu(values) + 1.0


def recv_from(v, axis, k):
    n = lax.axis_size(axis)
    return lax.ppermute(v, axis, [(i, (i + k) % n) for i in range(n)])


def line_prefix(v, axis, held=None):
    n = lax.axis_size(axis)
    me = lax.axis_index(axis)
    sent = v.astype(jnp.bfloat16)
    got = [recv_from(sent, axis, k) for k in range(1, n)]
    got, held = lax.optimization_barrier((got, held))
    before = jnp.zeros_like(v)
    total = v
    for k, g in enumerate(got, start=1):
        g = g.astype(v.dtype)
        before = before + jnp.where(k <= me, g, jnp.zeros_like(g))
        total = total + g
    return before, total, held


def exclusive_rows_scan(states, inputs, x_work, y_work):
    core = lax.axis_index("core")
    other = recv_from(states, "core", 1)
    other, inputs = lax.optimization_barrier((other, inputs))
    xdone = x_work(*inputs)
    total = states + other
    own = jnp.where(core == 1, other, jnp.zeros_like(other))
    half = total.shape[0] // 2
    mine = lax.dynamic_slice_in_dim(total, core * half, half, axis=0)
    xpre, xsum, xdone = line_prefix(mine, "x", xdone)
    ydone = y_work(*xdone)
    ypre, _, ydone = line_prefix(xsum, "y", ydone)
    part = ypre + xpre
    part_other = recv_from(part, "core", 1)
    lo = jnp.where(core == 0, part, part_other)
    hi = jnp.where(core == 0, part_other, part)
    return jnp.concatenate([lo, hi], axis=0) + own, ydone


def ring_gather(x, axis):
    n = lax.axis_size(axis)
    fwd = bwd = x
    got = {0: x}
    for s in range(1, (n + 1) // 2):
        fwd = recv_from(fwd, axis, 1)
        bwd = recv_from(bwd, axis, n - 1)
        got[n - s] = fwd
        got[s] = bwd
    if n % 2 == 0 and n > 1:
        h = x.shape[1] // 2
        a = recv_from(fwd[:, :h], axis, 1)
        b = recv_from(bwd[:, h:], axis, n - 1)
        got[n // 2] = jnp.concatenate([a, b], axis=1)
    return [got[d] for d in range(n)]


def to_owners(res):
    n = lax.axis_size("cols")
    g = lax.axis_index("cols")
    blocks = res.reshape(n, res.shape[0] // n, *res.shape[1:])
    out = [(g, blocks[0])]
    for k in range(1, n):
        out.append(((g - k) % n, recv_from(blocks[k], "cols", k)))
    return out


def body(sheet, w_in, w_out):
    high = lax.Precision.HIGHEST
    width = sheet.shape[2]
    heads_here = w_in.shape[1]
    hdim = w_out.shape[1] // 2
    core = lax.axis_index("core")

    xloc = sheet.astype(jnp.float32)
    normed = (xloc * lax.rsqrt(jnp.mean(xloc * xloc, axis=-1, keepdims=True) + 1e-06)).astype(jnp.bfloat16)
    shards = ring_gather(normed, "cols")

    shards, w_held = lax.optimization_barrier((shards, w_out))
    w_pair = lax.all_gather(w_held, "cols")

    row_count = normed.shape[1]

    def project_in(x, lo, hi):
        w = w_in[:, :, lo * hdim : hi * hdim].reshape(width, -1)
        out = jnp.dot(x.reshape(-1, width), w, preferred_element_type=jnp.float32)
        return out.reshape(x.shape[0], row_count, heads_here, hi - lo, hdim)

    pc = jnp.concatenate([project_in(s, 4, 6) for s in shards], axis=0)
    fk = feature_map(pc[..., 0, :]).astype(jnp.bfloat16)
    vcol = pc[..., 1, :].astype(jnp.bfloat16)
    states = jnp.einsum("crhk,crhv->chkv", fk, vcol, preferred_element_type=jnp.float32)
    scale = hdim ** (-0.5)
    causal = (jnp.arange(row_count)[:, None] >= jnp.arange(row_count)[None, :]).astype(jnp.float32)

    def rest(*parts):
        pr = project_in(jnp.concatenate(parts, axis=0), 0, 4)
        qrow = head_norm(pr[..., 0, :]).astype(jnp.bfloat16)
        krow = head_norm(pr[..., 1, :]).astype(jnp.bfloat16)
        vrow = pr[..., 2, :].astype(jnp.bfloat16)
        fq = feature_map(pr[..., 3, :]).astype(jnp.bfloat16)
        inner = jnp.einsum("cthd,cshd->chts", fq, fk, preferred_element_type=jnp.float32) * causal
        local = jnp.einsum("chts,cshv->cthv", inner, vcol.astype(jnp.float32), precision=high)
        return qrow, krow, vrow, fq, local

    def row_attention(qrow, krow, vrow, fq, local):
        q32, k32, v32 = (t.astype(jnp.float32) for t in (qrow, krow, vrow))
        score = jnp.sum(q32[:, None] * k32[None], axis=-1) * scale
        expo = jnp.exp(score)
        weights = (expo / jnp.sum(expo, axis=1, keepdims=True)).astype(jnp.bfloat16)
        orow = jnp.sum(weights.astype(jnp.float32)[..., None] * v32[None], axis=1).astype(jnp.bfloat16)
        return orow, fq, local

    prior, (orow, fq, local) = exclusive_rows_scan(states, tuple(shards), rest, row_attention)

    carried = jnp.einsum("cthk,chkv->cthv", fq.astype(jnp.float32), prior, precision=high)
    ocol = head_norm(carried + local).astype(jnp.bfloat16)
    both = to_owners(jnp.concatenate([orow, ocol], axis=3))

    mixed = None
    for src_group, block in both:
        w = lax.dynamic_index_in_dim(w_pair, src_group, axis=0, keepdims=False)
        part = jnp.einsum("crhf,hfn->crn", block, w, preferred_element_type=jnp.float32)
        mixed = part if mixed is None else mixed + part
    return mixed.astype(jnp.bfloat16)


def split_mesh(mesh):
    devs = mesh.devices
    n_rows, n_cols = devs.shape
    try:
        nx = len({d.coords[0] for d in devs.flat})
    except Exception:
        nx = 4
    ny = n_rows // (nx * 2)
    return Mesh(devs.reshape(ny, nx, 2, n_cols), ROWS_AXES + ("cols",))


def solution(mesh):
    m4 = split_mesh(mesh)
    spec = P("cols", ROWS_AXES, None)
    return jax.shard_map(
        body,
        mesh=m4,
        in_specs=(spec, P(None, "cols", None), P("cols", None, None)),
        out_specs=spec,
        check_vma=False,
    )
```

```python
import jax
import jax.numpy as jnp
import numpy as np
from jax import lax
from jax.sharding import Mesh, PartitionSpec as P

ROWS_AXES = ("y", "x", "core")


def head_norm(values):
    return values * lax.rsqrt(jnp.mean(values * values, axis=-1, keepdims=True) + 1e-06)


def feature_map(values):
    return jax.nn.elu(values) + 1.0


def recv_from(v, axis, k):
    n = lax.axis_size(axis)
    return lax.ppermute(v, axis, [(i, (i + k) % n) for i in range(n)])


def line_prefix(v, axis, held=None):
    n = lax.axis_size(axis)
    me = lax.axis_index(axis)
    sent = v.astype(jnp.bfloat16)
    got = [recv_from(sent, axis, k) for k in range(1, n)]
    got, held = lax.optimization_barrier((got, held))
    before = jnp.zeros_like(v)
    total = v
    for k, g in enumerate(got, start=1):
        g = g.astype(v.dtype)
        before = before + jnp.where(k <= me, g, jnp.zeros_like(g))
        total = total + g
    return before, total, held


def exclusive_rows_scan(states, inputs, x_work, y_work):
    core = lax.axis_index("core")
    other = recv_from(states, "core", 1)
    other, inputs = lax.optimization_barrier((other, inputs))
    xdone = x_work(*inputs)
    total = states + other
    own = jnp.where(core == 1, other, jnp.zeros_like(other))
    half = total.shape[0] // 2
    mine = lax.dynamic_slice_in_dim(total, core * half, half, axis=0)
    xpre, xsum, xdone = line_prefix(mine, "x", xdone)
    ydone = y_work(*xdone)
    ypre, _, ydone = line_prefix(xsum, "y", ydone)
    part = ypre + xpre
    part_other = recv_from(part, "core", 1)
    lo = jnp.where(core == 0, part, part_other)
    hi = jnp.where(core == 0, part_other, part)
    return jnp.concatenate([lo, hi], axis=0) + own, ydone


def ring_gather(x, axis, held):
    n = lax.axis_size(axis)
    fwd = bwd = x
    got = {0: x}
    for s in range(1, (n + 1) // 2):
        fwd = recv_from(fwd, axis, 1)
        bwd = recv_from(bwd, axis, n - 1)
        if s == 1:
            fwd, bwd, held = lax.optimization_barrier((fwd, bwd, held))
        got[n - s] = fwd
        got[s] = bwd
    if n % 2 == 0 and n > 1:
        h = x.shape[1] // 2
        a = recv_from(fwd[:, :h], axis, 1)
        b = recv_from(bwd[:, h:], axis, n - 1)
        got[n // 2] = jnp.concatenate([a, b], axis=1)
    return jnp.concatenate([got[d] for d in range(n)], axis=0), held


def to_owners(res):
    n = lax.axis_size("cols")
    g = lax.axis_index("cols")
    blocks = res.reshape(n, res.shape[0] // n, *res.shape[1:])
    out = [(g, blocks[0])]
    for k in range(1, n):
        out.append(((g - k) % n, recv_from(blocks[k], "cols", k)))
    return out


def body(sheet, w_in, w_out):
    high = lax.Precision.HIGHEST
    width = sheet.shape[2]
    heads_here = w_in.shape[1]
    hdim = w_out.shape[1] // 2
    core = lax.axis_index("core")

    xloc = sheet.astype(jnp.float32)
    normed = (xloc * lax.rsqrt(jnp.mean(xloc * xloc, axis=-1, keepdims=True) + 1e-06)).astype(jnp.bfloat16)
    w_rest = w_in[:, :, : 4 * hdim]
    piece, w_rest = ring_gather(normed, "cols", w_rest)

    piece, w_held = lax.optimization_barrier((piece, w_out))
    w_pair = lax.all_gather(w_held, "cols")

    all_cols, row_count = piece.shape[0], piece.shape[1]

    def project_in(x, lo, hi):
        w = (w_rest if lo == 0 else w_in[:, :, lo * hdim : hi * hdim]).reshape(width, -1)
        out = jnp.dot(x.reshape(-1, width), w, preferred_element_type=jnp.float32)
        return out.reshape(all_cols, row_count, heads_here, hi - lo, hdim)

    pc = project_in(piece, 4, 6)
    fk = feature_map(pc[..., 0, :]).astype(jnp.bfloat16)
    vcol = pc[..., 1, :].astype(jnp.bfloat16)
    states = jnp.einsum("crhk,crhv->chkv", fk, vcol, preferred_element_type=jnp.float32)
    scale = hdim ** (-0.5)
    causal = (jnp.arange(row_count)[:, None] >= jnp.arange(row_count)[None, :]).astype(jnp.float32)

    def rest(x):
        pr = project_in(x, 0, 4)
        qrow = head_norm(pr[..., 0, :]).astype(jnp.bfloat16)
        krow = head_norm(pr[..., 1, :]).astype(jnp.bfloat16)
        vrow = pr[..., 2, :].astype(jnp.bfloat16)
        fq = feature_map(pr[..., 3, :]).astype(jnp.bfloat16)
        inner = jnp.einsum("cthd,cshd->chts", fq, fk, preferred_element_type=jnp.float32) * causal
        local = jnp.einsum("chts,cshv->cthv", inner, vcol.astype(jnp.float32), precision=high)
        return qrow, krow, vrow, fq, local

    def row_attention(qrow, krow, vrow, fq, local):
        q32, k32, v32 = (t.astype(jnp.float32) for t in (qrow, krow, vrow))
        score = jnp.sum(q32[:, None] * k32[None], axis=-1) * scale
        expo = jnp.exp(score)
        weights = (expo / jnp.sum(expo, axis=1, keepdims=True)).astype(jnp.bfloat16)
        orow = jnp.sum(weights.astype(jnp.float32)[..., None] * v32[None], axis=1).astype(jnp.bfloat16)
        return orow, fq, local

    prior, (orow, fq, local) = exclusive_rows_scan(states, (piece,), rest, row_attention)

    carried = jnp.einsum("cthk,chkv->cthv", fq.astype(jnp.float32), prior, precision=high)
    ocol = head_norm(carried + local).astype(jnp.bfloat16)
    both = to_owners(jnp.concatenate([orow, ocol], axis=3))

    mixed = None
    for src_group, block in both:
        w = lax.dynamic_index_in_dim(w_pair, src_group, axis=0, keepdims=False)
        part = jnp.einsum("crhf,hfn->crn", block, w, preferred_element_type=jnp.float32)
        mixed = part if mixed is None else mixed + part
    return mixed.astype(jnp.bfloat16)


def split_mesh(mesh):
    devs = mesh.devices
    n_rows, n_cols = devs.shape
    try:
        nx = len({d.coords[0] for d in devs.flat})
    except Exception:
        nx = 4
    ny = n_rows // (nx * 2)
    return Mesh(devs.reshape(ny, nx, 2, n_cols), ROWS_AXES + ("cols",))


def solution(mesh):
    m4 = split_mesh(mesh)
    spec = P("cols", ROWS_AXES, None)
    return jax.shard_map(
        body,
        mesh=m4,
        in_specs=(spec, P(None, "cols", None), P("cols", None, None)),
        out_specs=spec,
        check_vma=False,
    )
```

```python
import jax
import jax.numpy as jnp
import numpy as np
from jax import lax
from jax.sharding import Mesh, PartitionSpec as P

ROWS_AXES = ("y", "x", "core")


def head_norm(values):
    return values * lax.rsqrt(jnp.mean(values * values, axis=-1, keepdims=True) + 1e-06)


def feature_map(values):
    return jax.nn.elu(values) + 1.0


def recv_from(v, axis, k):
    n = lax.axis_size(axis)
    return lax.ppermute(v, axis, [(i, (i + k) % n) for i in range(n)])


def line_prefix(v, axis, held=None):
    n = lax.axis_size(axis)
    me = lax.axis_index(axis)
    sent = v.astype(jnp.bfloat16)
    got = [recv_from(sent, axis, k) for k in range(1, n)]
    got, held = lax.optimization_barrier((got, held))
    before = jnp.zeros_like(v)
    total = v
    for k, g in enumerate(got, start=1):
        g = g.astype(v.dtype)
        before = before + jnp.where(k <= me, g, jnp.zeros_like(g))
        total = total + g
    return before, total, held


def exclusive_rows_scan(states, inputs, x_work, y_work):
    core = lax.axis_index("core")
    other = recv_from(states, "core", 1)
    other, inputs = lax.optimization_barrier((other, inputs))
    xdone = x_work(*inputs)
    total = states + other
    own = jnp.where(core == 1, other, jnp.zeros_like(other))
    half = total.shape[0] // 2
    mine = lax.dynamic_slice_in_dim(total, core * half, half, axis=0)
    xpre, xsum, xdone = line_prefix(mine, "x", xdone)
    ydone = y_work(*xdone)
    ypre, _, ydone = line_prefix(xsum, "y", ydone)
    part = ypre + xpre
    part_other = recv_from(part, "core", 1)
    lo = jnp.where(core == 0, part, part_other)
    hi = jnp.where(core == 0, part_other, part)
    return jnp.concatenate([lo, hi], axis=0) + own, ydone


def ring_gather(x, axis, held):
    n = lax.axis_size(axis)
    fwd = bwd = x
    got = {0: x}
    for s in range(1, (n + 1) // 2):
        fwd = recv_from(fwd, axis, 1)
        bwd = recv_from(bwd, axis, n - 1)
        if s == 1:
            fwd, bwd, held = lax.optimization_barrier((fwd, bwd, held))
        got[n - s] = fwd
        got[s] = bwd
    if n % 2 == 0 and n > 1:
        h = x.shape[1] // 2
        a = recv_from(fwd[:, :h], axis, 1)
        b = recv_from(bwd[:, h:], axis, n - 1)
        got[n // 2] = jnp.concatenate([a, b], axis=1)
    return jnp.concatenate([got[d] for d in range(n)], axis=0), held


def to_owners(res):
    n = lax.axis_size("cols")
    g = lax.axis_index("cols")
    blocks = res.reshape(n, res.shape[0] // n, *res.shape[1:])
    out = [(g, blocks[0])]
    for k in range(1, n):
        out.append(((g - k) % n, recv_from(blocks[k], "cols", k)))
    return out


def body(sheet, w_in, w_out):
    high = lax.Precision.HIGHEST
    width = sheet.shape[2]
    heads_here = w_in.shape[1]
    hdim = w_out.shape[1] // 2
    core = lax.axis_index("core")

    xloc = sheet.astype(jnp.float32)
    normed = (xloc * lax.rsqrt(jnp.mean(xloc * xloc, axis=-1, keepdims=True) + 1e-06)).astype(jnp.bfloat16)
    w_rest = w_in[:, :, : 4 * hdim].reshape(width, -1)
    piece, w_rest = ring_gather(normed, "cols", w_rest)

    piece, w_held = lax.optimization_barrier((piece, w_out))
    w_pair = lax.all_gather(w_held, "cols")

    all_cols, row_count = piece.shape[0], piece.shape[1]

    def project_in(x, lo, hi):
        w = w_rest if lo == 0 else w_in[:, :, lo * hdim : hi * hdim].reshape(width, -1)
        out = jnp.dot(x.reshape(-1, width), w, preferred_element_type=jnp.float32)
        return out.reshape(all_cols, row_count, heads_here, hi - lo, hdim)

    pc = project_in(piece, 4, 6)
    fk = feature_map(pc[..., 0, :]).astype(jnp.bfloat16)
    vcol = pc[..., 1, :].astype(jnp.bfloat16)
    states = jnp.einsum("crhk,crhv->chkv", fk, vcol, preferred_element_type=jnp.float32)
    scale = hdim ** (-0.5)
    causal = (jnp.arange(row_count)[:, None] >= jnp.arange(row_count)[None, :]).astype(jnp.float32)

    def rest(x):
        pr = project_in(x, 0, 4)
        qrow = head_norm(pr[..., 0, :]).astype(jnp.bfloat16)
        krow = head_norm(pr[..., 1, :]).astype(jnp.bfloat16)
        vrow = pr[..., 2, :].astype(jnp.bfloat16)
        fq = feature_map(pr[..., 3, :]).astype(jnp.bfloat16)
        inner = jnp.einsum("cthd,cshd->chts", fq, fk, preferred_element_type=jnp.float32) * causal
        local = jnp.einsum("chts,cshv->cthv", inner, vcol.astype(jnp.float32), precision=high)
        return qrow, krow, vrow, fq, local

    def row_attention(qrow, krow, vrow, fq, local):
        q32, k32, v32 = (t.astype(jnp.float32) for t in (qrow, krow, vrow))
        score = jnp.sum(q32[:, None] * k32[None], axis=-1) * scale
        expo = jnp.exp(score)
        weights = (expo / jnp.sum(expo, axis=1, keepdims=True)).astype(jnp.bfloat16)
        orow = jnp.sum(weights.astype(jnp.float32)[..., None] * v32[None], axis=1).astype(jnp.bfloat16)
        return orow, fq, local

    prior, (orow, fq, local) = exclusive_rows_scan(states, (piece,), rest, row_attention)

    carried = jnp.einsum("cthk,chkv->cthv", fq.astype(jnp.float32), prior, precision=high)
    ocol = head_norm(carried + local).astype(jnp.bfloat16)
    both = to_owners(jnp.concatenate([orow, ocol], axis=3))

    mixed = None
    for src_group, block in both:
        w = lax.dynamic_index_in_dim(w_pair, src_group, axis=0, keepdims=False)
        part = jnp.einsum("crhf,hfn->crn", block, w, preferred_element_type=jnp.float32)
        mixed = part if mixed is None else mixed + part
    return mixed.astype(jnp.bfloat16)


def split_mesh(mesh):
    devs = mesh.devices
    n_rows, n_cols = devs.shape
    try:
        nx = len({d.coords[0] for d in devs.flat})
    except Exception:
        nx = 4
    ny = n_rows // (nx * 2)
    return Mesh(devs.reshape(ny, nx, 2, n_cols), ROWS_AXES + ("cols",))


def solution(mesh):
    m4 = split_mesh(mesh)
    spec = P("cols", ROWS_AXES, None)
    return jax.shard_map(
        body,
        mesh=m4,
        in_specs=(spec, P(None, "cols", None), P("cols", None, None)),
        out_specs=spec,
        check_vma=False,
    )
```
